512 devices in a mesh: node: 32 (over z, core), feat: 16 (over x, y).
Axes of the slice: x: 4, y: 4, z: 16, core: 2. Of those that a mesh axis runs over, the one named last changes fastest.
Arguments:
- covariates: bfloat16 [256, 131072], P('feat', 'node'), may hold values from 0 to 0.9921875
- pseudo: bfloat16 [16, 131072], P(None, 'node'), may hold values from -6 to 6
- honest: int32 [131072], P('node'), may hold values 0 or 1
- destination: int32 [131072, 1], P('node'), may hold values from 0 to 63; in each aligned block of 4096 rows (0 to 4095, 4096 to 8191, ...) at most 128 rows name the same one
- node_slot: int32 [64], replicated, may hold values from 0 to 63, each once
Outputs:
- histogram: float32 [64, 256, 17, 256], P('node', 'feat')
- best_gain: float32 [64], P('node')
The draws below stay inside these ranges and needn't reach their ends.
Inputs may be any that keep to these rules, and one draw needn't show every extreme that they name: `destination`: in the rows of one device no child node is named by more than 128 rows. Each slot appears once; child node n belongs to the owner node_slot[n] // 2 along node.
All inputs are finite; a program needn't handle non-finite values. No bound on the sum of `honest` on one device may be relied on, other than what follows from the above.
Results may differ from the reference program's by a relative error of at most 0.0003.
Values may be sent and summed in bfloat16 or wider, within the bound.
No kernel may reach another device: no remote copies, remote signals or barrier semaphores. Data moves between devices by JAX's collectives and lax.ppermute only.
A program may use at most 64 MiB of HBM per device.

```python
import math
import jax
import jax.numpy as jnp
import numpy as np
from jax import lax

F = 256
B = 256
PSEUDO = 16
ROWS_DEV = 4096
ROWS = 131072
NODES = 64
MOST = 128


def with_ends(drawn, rng, low, largest):
    place = [jax.random.randint(jax.random.fold_in(rng, axis), (), 0, length) for axis, length in enumerate(drawn.shape)]
    longest = drawn.shape.index(max(drawn.shape))
    neighbour = place[:longest] + [(place[longest] + 1) % drawn.shape[longest]] + place[longest + 1:]
    return drawn.at[tuple(place)].set(low).at[tuple(neighbour)].set(largest)


def level_of(key, shape, shards, least, top_value):
    loudness = 1.0
    for dim, shards_of in shards:
        steps = jax.random.uniform(jax.random.fold_in(jax.random.fold_in(key, 6), dim), (shards_of,), jnp.float32, least / len(shards), top_value / len(shards))
        loudness = loudness * jnp.repeat(jnp.exp(steps), shape[dim] // shards_of).reshape((-1,) + (1,) * (len(shape) - 1 - dim))
    return loudness


def shared_out(own_key, own, number, rows, number_of, top, bound, skew):
    order = jax.random.permutation(own_key, number_of)
    heavy_load, common = shares(number_of, rows * top, bound, skew, True), shares(number_of, rows * top, bound, skew, False)
    places = jnp.arange(number_of)

    def named(sizes, turn):
        used = int((sizes > 0).sum())
        fixed = max(1, used // 4)
        moved = fixed + (places - fixed + turn * (used - fixed)) % max(1, number_of - fixed)
        return jnp.zeros((number_of,), jnp.int32).at[order[jnp.where(places < fixed, places, moved)]].set(jnp.asarray(sizes, jnp.int32))

    sizes = jnp.where(number % 4 == 0, named(heavy_load, number // 4), named(common, number - number // 4 - 1))
    mixed = jax.random.permutation(jax.random.fold_in(own, 3), number_of)
    source_of, receiver = mixed[0:number_of // 2 * 2:2], mixed[1:number_of // 2 * 2:2]
    slack = jnp.minimum(sizes[source_of] - 1, bound - sizes[receiver]) // 2
    slack = jnp.where((source_of == order[0]) | (receiver == order[0]) | (sizes[receiver] == 0), 0, jnp.maximum(slack, 0))
    moved = jax.random.randint(jax.random.fold_in(own, 4), (number_of // 2,), 0, 1 << 20) % (slack + 1)
    sizes = sizes.at[source_of].add(-moved).at[receiver].add(moved)
    labels = jnp.searchsorted(jnp.cumsum(sizes), jnp.arange(rows * top), side="right").astype(jnp.int32)
    listing = labels.reshape(top, rows).T
    listing = listing[jax.random.permutation(jax.random.fold_in(own, 1), rows)]
    turn = jax.random.randint(jax.random.fold_in(own, 2), (rows, 1), 0, top)
    return jnp.take_along_axis(listing, (jnp.arange(top)[None, :] + turn) % top, axis=1)


def shares(count, total, reach, lean, full):
    weights = [(1 << 20) // math.isqrt(grade ** lean) + 1 for grade in range(1, count + 1)]
    largest = reach if full else min(reach, max(-(-total // count), total * weights[0] // sum(weights)))
    least = 1 if total - largest >= count - 1 else 0
    given, rest = [largest] + [least] * (count - 1), total - largest - least * (count - 1)
    while rest > 0:
        movable = [i for i in range(1, count) if given[i] < largest] or [i for i in range(1, count) if given[i] < reach]
        mass, budget = sum([weights[i] for i in movable]), rest
        for i in movable:
            extra = min(reach - given[i], max(1, budget * weights[i] // mass), rest)
            given[i] = given[i] + extra
            rest = rest - extra
    return np.array(given)


def bell_draw(stream_key, shape, width, bound, pieces=(), dtype=jnp.bfloat16):
    values = width * jax.random.normal(stream_key, shape, jnp.float32)
    if pieces:
        values = values * level_of(stream_key, shape, pieces, -0.22, 0.18)
    return jnp.clip(values, -bound, bound).astype(dtype)


def setup_inputs(seed: int = 0) -> dict:
    keys = jax.random.split(jax.random.key(seed), 6)
    covariates = jnp.clip(0.9921875 * jax.random.uniform(keys[0], (F, ROWS), jnp.float32) ** level_of(keys[0], (F, ROWS), ((0, 16), (1, 32)), -0.2, 0.2), 0.0, 0.9921875).astype(jnp.bfloat16)
    pseudo = bell_draw(keys[1], (PSEUDO, ROWS), 1.0, 6.0, ((1, 32),))
    honest = with_ends((jax.random.randint(keys[2], (ROWS,), 0, 2) < 1).astype(jnp.int32), jax.random.fold_in(keys[2], 1), 0, 1)
    destination_keys = jax.random.split(jax.random.fold_in(keys[3], 1), ROWS // ROWS_DEV)
    destination_turns = jax.random.permutation(jax.random.fold_in(keys[3], 3), ROWS // ROWS_DEV)
    destination = jax.vmap(lambda own, number: shared_out(jax.random.fold_in(keys[3], 2), own, number, ROWS_DEV, NODES, 1, MOST, 2))(destination_keys, destination_turns).reshape((ROWS, 1))
    node_slot = jax.random.permutation(keys[4], NODES).astype(jnp.int32)
    return {"covariates": covariates, "pseudo": pseudo, "honest": honest, "destination": destination, "node_slot": node_slot}


def reference(covariates, pseudo, honest, destination, node_slot):
    bins = jnp.floor(covariates.astype(jnp.float32) * B).astype(jnp.int32)
    weight = (1 - honest).astype(jnp.float32)
    statistics = jnp.concatenate([weight[None, :], weight[None, :] * pseudo.astype(jnp.float32)], axis=0)
    target = node_slot[destination[:, 0]].astype(jnp.int32)
    stat_rows = jnp.transpose(statistics)

    def per_feature(bin_row):
        segment = target * B + bin_row
        return jax.ops.segment_sum(stat_rows, segment, num_segments=NODES * B)

    stacked = lax.map(per_feature, bins)
    histogram = jnp.transpose(stacked.reshape(F, NODES, B, PSEUDO + 1), (1, 0, 3, 2))
    left = jnp.cumsum(histogram, axis=3)
    total = left[:, :, :, -1:]
    right = total - left
    left_part = jnp.sum(left[:, :, 1:] * left[:, :, 1:], axis=2) / (left[:, :, 0] + 1.0)
    right_part = jnp.sum(right[:, :, 1:] * right[:, :, 1:], axis=2) / (right[:, :, 0] + 1.0)
    total_part = jnp.sum(total[:, :, 1:] * total[:, :, 1:], axis=2) / (total[:, :, 0] + 1.0)
    gain = left_part + right_part - total_part
    best_gain = jnp.max(gain, axis=(1, 2))
    return histogram, best_gain
```

```python
import jax
import jax.numpy as jnp
from jax import lax
from jax.sharding import PartitionSpec as P

B = 256
BLOCK = 256


def feature_histograms(bin_table, statistics):
    levels = lax.broadcasted_iota(jnp.int32, (1, 1, B), 2)

    def one_feature(bin_row):
        indicator = (bin_row[:, :, None] == levels).astype(jnp.bfloat16)
        return jnp.einsum("skr,krb->ksb", statistics, indicator, preferred_element_type=jnp.float32)

    stacked = lax.map(one_feature, bin_table)
    return jnp.transpose(stacked, (1, 0, 2, 3))


def running_rank(owned):
    rows, nodes = owned.shape
    blocks = rows // BLOCK
    ob = owned.reshape(blocks, BLOCK, nodes).astype(jnp.bfloat16)
    i = lax.broadcasted_iota(jnp.int32, (BLOCK, BLOCK), 0)
    j = lax.broadcasted_iota(jnp.int32, (BLOCK, BLOCK), 1)
    lower = (i >= j).astype(jnp.bfloat16)
    within = jnp.einsum("ij,bjn->bin", lower, ob, preferred_element_type=jnp.float32)
    totals = within[:, -1, :]
    a = lax.broadcasted_iota(jnp.int32, (blocks, blocks), 0)
    c = lax.broadcasted_iota(jnp.int32, (blocks, blocks), 1)
    before = (a > c).astype(jnp.float32)
    prefix = jnp.einsum("ac,cn->an", before, totals, precision=lax.Precision.HIGHEST)
    counts = within + prefix[:, None, :]
    mine = jnp.sum(counts * ob.astype(jnp.float32), axis=2).reshape(rows)
    return mine.astype(jnp.int32) - 1


def on_device(covariates, pseudo, honest, destination, node_slot):
    feat_count, row_count = covariates.shape
    node_devices = lax.axis_size("node")
    feat_devices = lax.axis_size("feat")
    node_total = node_slot.shape[0]
    node_local = node_total // node_devices
    capacity = 2 * row_count // node_total
    weight = (1 - honest).astype(jnp.float32)
    columns = lax.broadcasted_iota(jnp.int32, (1, node_total), 1)
    named = (destination == columns).astype(jnp.int32)
    target = jnp.sum(named * node_slot[None, :], axis=1)
    owned = (target[:, None] == columns).astype(jnp.int32)
    rank = running_rank(owned)
    position = target * capacity + rank
    weighted = weight[None, :] * pseudo.astype(jnp.float32)
    weight_row = weight[None, :].astype(jnp.bfloat16)
    payload = jnp.concatenate([covariates, weight_row, weighted.astype(jnp.bfloat16)], axis=0)
    payload_width = payload.shape[0]
    outgoing = (
        jnp.zeros((payload_width, node_total * capacity), jnp.bfloat16).at[:, position].set(payload)
    )
    outgoing = outgoing.reshape(payload_width, node_devices, node_local, capacity)
    arrived = lax.all_to_all(outgoing, "node", split_axis=1, concat_axis=3, tiled=True)[:, 0]
    bin_table = jnp.floor(arrived[:feat_count].astype(jnp.float32) * B).astype(jnp.int32)
    statistics = arrived[feat_count:]
    histogram = feature_histograms(bin_table, statistics)
    c = lax.broadcasted_iota(jnp.int32, (B, B), 0)
    b = lax.broadcasted_iota(jnp.int32, (B, B), 1)
    upper = (c <= b).astype(jnp.float32)
    left = jnp.einsum("nfsc,cb->nfsb", histogram, upper, precision=lax.Precision.HIGHEST)
    total = left[:, :, :, -1:]
    right = total - left
    left_part = jnp.sum(left[:, :, 1:] * left[:, :, 1:], axis=2) / (left[:, :, 0] + 1.0)
    right_part = jnp.sum(right[:, :, 1:] * right[:, :, 1:], axis=2) / (right[:, :, 0] + 1.0)
    total_part = jnp.sum(total[:, :, 1:] * total[:, :, 1:], axis=2) / (total[:, :, 0] + 1.0)
    gain = left_part + right_part - total_part
    best_local = jnp.max(gain, axis=(1, 2))
    spread = jnp.broadcast_to(best_local[None, :], (feat_devices, node_local))
    gathered = lax.all_to_all(spread, "feat", split_axis=0, concat_axis=0, tiled=True)
    best_gain = jnp.max(gathered, axis=0)
    return (histogram, best_gain)


def solution(mesh):
    placed = (P("feat", "node"), P(None, "node"), P("node"), P("node", None), P())
    return jax.shard_map(
        on_device,
        mesh=mesh,
        in_specs=placed,
        out_specs=(P("node", "feat", None, None), P("node")),
        check_vma=False,
    )
```

```python
import jax
import jax.numpy as jnp
from jax import lax
from jax.sharding import PartitionSpec as P

B = 256
BLOCK = 256


def feature_histograms(bin_table, statistics):
    levels = lax.broadcasted_iota(jnp.int32, (1, 1, 1, B), 3)
    indicator = (bin_table[:, :, :, None] == levels).astype(jnp.bfloat16)
    return jnp.einsum("skr,fkrb->kfsb", statistics, indicator, preferred_element_type=jnp.float32)


def running_rank(owned):
    rows, nodes = owned.shape
    blocks = rows // BLOCK
    ob = owned.reshape(blocks, BLOCK, nodes).astype(jnp.bfloat16)
    i = lax.broadcasted_iota(jnp.int32, (BLOCK, BLOCK), 0)
    j = lax.broadcasted_iota(jnp.int32, (BLOCK, BLOCK), 1)
    lower = (i >= j).astype(jnp.bfloat16)
    within = jnp.einsum("ij,bjn->bin", lower, ob, preferred_element_type=jnp.float32)
    totals = within[:, -1, :]
    a = lax.broadcasted_iota(jnp.int32, (blocks, blocks), 0)
    c = lax.broadcasted_iota(jnp.int32, (blocks, blocks), 1)
    before = (a > c).astype(jnp.float32)
    prefix = jnp.einsum("ac,cn->an", before, totals, precision=lax.Precision.HIGHEST)
    counts = within + prefix[:, None, :]
    mine = jnp.sum(counts * ob.astype(jnp.float32), axis=2).reshape(rows)
    return mine.astype(jnp.int32) - 1


def on_device(covariates, pseudo, honest, destination, node_slot):
    feat_count, row_count = covariates.shape
    node_devices = lax.axis_size("node")
    feat_devices = lax.axis_size("feat")
    node_total = node_slot.shape[0]
    node_local = node_total // node_devices
    capacity = 2 * row_count // node_total
    weight = (1 - honest).astype(jnp.float32)
    columns = lax.broadcasted_iota(jnp.int32, (1, node_total), 1)
    named = (destination == columns).astype(jnp.int32)
    target = jnp.sum(named * node_slot[None, :], axis=1)
    owned = (target[:, None] == columns).astype(jnp.int32)
    rank = running_rank(owned)
    position = target * capacity + rank
    weighted = weight[None, :] * pseudo.astype(jnp.float32)
    weight_row = weight[None, :].astype(jnp.bfloat16)
    payload = jnp.concatenate([covariates, weight_row, weighted.astype(jnp.bfloat16)], axis=0)
    payload_width = payload.shape[0]
    outgoing = (
        jnp.zeros((payload_width, node_total * capacity), jnp.bfloat16).at[:, position].set(payload)
    )
    outgoing = outgoing.reshape(payload_width, node_devices, node_local, capacity)
    half = feat_count // 2
    first = jnp.concatenate([outgoing[feat_count:], outgoing[:half]], axis=0)
    second = outgoing[half:feat_count]
    stat_count = payload_width - feat_count
    arrived_a = lax.all_to_all(first, "node", split_axis=1, concat_axis=3, tiled=True)[:, 0]
    arrived_b = lax.all_to_all(second, "node", split_axis=1, concat_axis=3, tiled=True)[:, 0]
    statistics = arrived_a[:stat_count]
    bins_a = jnp.floor(arrived_a[stat_count:].astype(jnp.float32) * B).astype(jnp.int32)
    hist_a = feature_histograms(bins_a, statistics)
    bins_b = jnp.floor(arrived_b.astype(jnp.float32) * B).astype(jnp.int32)
    hist_b = feature_histograms(bins_b, statistics)
    histogram = jnp.concatenate([hist_a, hist_b], axis=1)
    c = lax.broadcasted_iota(jnp.int32, (B, B), 0)
    b = lax.broadcasted_iota(jnp.int32, (B, B), 1)
    upper = (c <= b).astype(jnp.float32)
    left = jnp.einsum("nfsc,cb->nfsb", histogram, upper, precision=lax.Precision.HIGHEST)
    total = left[:, :, :, -1:]
    right = total - left
    left_part = jnp.sum(left[:, :, 1:] * left[:, :, 1:], axis=2) / (left[:, :, 0] + 1.0)
    right_part = jnp.sum(right[:, :, 1:] * right[:, :, 1:], axis=2) / (right[:, :, 0] + 1.0)
    total_part = jnp.sum(total[:, :, 1:] * total[:, :, 1:], axis=2) / (total[:, :, 0] + 1.0)
    gain = left_part + right_part - total_part
    best_local = jnp.max(gain, axis=(1, 2))
    spread = jnp.broadcast_to(best_local[None, :], (feat_devices, node_local))
    gathered = lax.all_to_all(spread, "feat", split_axis=0, concat_axis=0, tiled=True)
    best_gain = jnp.max(gathered, axis=0)
    return (histogram, best_gain)


def solution(mesh):
    placed = (P("feat", "node"), P(None, "node"), P("node"), P("node", None), P())
    return jax.shard_map(
        on_device,
        mesh=mesh,
        in_specs=placed,
        out_specs=(P("node", "feat", None, None), P("node")),
        check_vma=False,
    )
```

```python
import jax
import jax.numpy as jnp
from jax import lax
from jax.sharding import PartitionSpec as P

B = 256
BLOCK = 256


def feature_histograms(bin_table, statistics):
    levels = lax.broadcasted_iota(jnp.int32, (1, 1, B), 2)

    def one_feature(bin_row):
        indicator = (bin_row[:, :, None] == levels).astype(jnp.bfloat16)
        return jnp.einsum("skr,krb->ksb", statistics, indicator, preferred_element_type=jnp.float32)

    stacked = lax.map(one_feature, bin_table)
    return jnp.transpose(stacked, (1, 0, 2, 3))


def running_rank(owned):
    rows, nodes = owned.shape
    blocks = rows // BLOCK
    ob = owned.reshape(blocks, BLOCK, nodes).astype(jnp.bfloat16)
    i = lax.broadcasted_iota(jnp.int32, (BLOCK, BLOCK), 0)
    j = lax.broadcasted_iota(jnp.int32, (BLOCK, BLOCK), 1)
    lower = (i >= j).astype(jnp.bfloat16)
    within = jnp.einsum("ij,bjn->bin", lower, ob, preferred_element_type=jnp.float32)
    totals = within[:, -1, :]
    a = lax.broadcasted_iota(jnp.int32, (blocks, blocks), 0)
    c = lax.broadcasted_iota(jnp.int32, (blocks, blocks), 1)
    before = (a > c).astype(jnp.float32)
    prefix = jnp.einsum("ac,cn->an", before, totals, precision=lax.Precision.HIGHEST)
    counts = within + prefix[:, None, :]
    mine = jnp.sum(counts * ob.astype(jnp.float32), axis=2).reshape(rows)
    return mine.astype(jnp.int32) - 1


def on_device(covariates, pseudo, honest, destination, node_slot):
    feat_count, row_count = covariates.shape
    node_devices = lax.axis_size("node")
    feat_devices = lax.axis_size("feat")
    node_total = node_slot.shape[0]
    node_local = node_total // node_devices
    capacity = 2 * row_count // node_total
    kept = honest == 0
    columns = lax.broadcasted_iota(jnp.int32, (1, node_total), 1)
    named = (destination == columns).astype(jnp.int32)
    target = jnp.sum(named * node_slot[None, :], axis=1)
    owned = ((target[:, None] == columns) & kept[:, None]).astype(jnp.int32)
    rank = running_rank(owned)
    slots = node_total * capacity
    position = jnp.where(kept, target * capacity + rank, slots)
    payload = jnp.concatenate([covariates, pseudo], axis=0)
    payload_width = payload.shape[0]
    empty = jnp.concatenate(
        [jnp.ones((feat_count, slots), jnp.bfloat16), jnp.zeros((payload_width - feat_count, slots), jnp.bfloat16)]
    )
    outgoing = empty.at[:, position].set(payload, mode="drop")
    outgoing = outgoing.reshape(payload_width, node_devices, node_local, capacity)
    arrived = lax.all_to_all(outgoing, "node", split_axis=1, concat_axis=3, tiled=True)[:, 0]
    bin_table = jnp.floor(arrived[:feat_count].astype(jnp.float32) * B).astype(jnp.int32)
    ones = jnp.ones((1,) + arrived.shape[1:], jnp.bfloat16)
    statistics = jnp.concatenate([ones, arrived[feat_count:]], axis=0)
    histogram = feature_histograms(bin_table, statistics)
    c = lax.broadcasted_iota(jnp.int32, (B, B), 0)
    b = lax.broadcasted_iota(jnp.int32, (B, B), 1)
    upper = (c <= b).astype(jnp.float32)
    left = jnp.einsum("nfsc,cb->nfsb", histogram, upper, precision=lax.Precision.HIGHEST)
    total = left[:, :, :, -1:]
    right = total - left
    left_part = jnp.sum(left[:, :, 1:] * left[:, :, 1:], axis=2) / (left[:, :, 0] + 1.0)
    right_part = jnp.sum(right[:, :, 1:] * right[:, :, 1:], axis=2) / (right[:, :, 0] + 1.0)
    total_part = jnp.sum(total[:, :, 1:] * total[:, :, 1:], axis=2) / (total[:, :, 0] + 1.0)
    gain = left_part + right_part - total_part
    best_local = jnp.max(gain, axis=(1, 2))
    spread = jnp.broadcast_to(best_local[None, :], (feat_devices, node_local))
    gathered = lax.all_to_all(spread, "feat", split_axis=0, concat_axis=0, tiled=True)
    best_gain = jnp.max(gathered, axis=0)
    return (histogram, best_gain)


def solution(mesh):
    placed = (P("feat", "node"), P(None, "node"), P("node"), P("node", None), P())
    return jax.shard_map(
        on_device,
        mesh=mesh,
        in_specs=placed,
        out_specs=(P("node", "feat", None, None), P("node")),
        check_vma=False,
    )
```

```python
import jax
import jax.numpy as jnp
from jax import lax
from jax.experimental import pallas as pl
from jax.experimental.pallas import tpu as pltpu
from jax.sharding import PartitionSpec as P

B = 256
BLOCK = 256
CH = 512


def histogram_kernel(bins_ref, stats_ref, hist_ref, best_ref):
    feats = bins_ref.shape[1]
    slots = bins_ref.shape[2]
    stat_count = stats_ref.shape[1]
    levels = lax.broadcasted_iota(jnp.int32, (B, CH), 0)
    c = lax.broadcasted_iota(jnp.int32, (B, B), 0)
    b = lax.broadcasted_iota(jnp.int32, (B, B), 1)
    upper = (c <= b).astype(jnp.bfloat16)
    best = jnp.full((1, B), -jnp.inf, jnp.float32)
    for f in range(feats):
        acc = jnp.zeros((stat_count, B), jnp.float32)
        for k in range(slots // CH):
            row = bins_ref[0, f:f + 1, k * CH:(k + 1) * CH]
            indicator = (levels == row).astype(jnp.bfloat16)
            acc = acc + lax.dot_general(
                stats_ref[0, :, k * CH:(k + 1) * CH], indicator, (((1,), (1,)), ((), ())),
                preferred_element_type=jnp.float32)
        hist_ref[0, f] = acc
    lane = lax.broadcasted_iota(jnp.int32, (stat_count, B), 1)
    for f in range(feats):
        left = hist_ref[0, f]
        shift = 1
        while shift < B:
            moved = pltpu.roll(left, shift, 1)
            left = left + jnp.where(lane >= shift, moved, 0.0)
            shift *= 2
        total = left[:, B - 1:B]
        right = total - left
        left_part = jnp.sum(left[1:] * left[1:], axis=0, keepdims=True) / (left[0:1] + 1.0)
        right_part = jnp.sum(right[1:] * right[1:], axis=0, keepdims=True) / (right[0:1] + 1.0)
        total_part = jnp.sum(total[1:] * total[1:], axis=0, keepdims=True) / (total[0:1] + 1.0)
        best = jnp.maximum(best, left_part + right_part - total_part)
    best_ref[0] = jnp.broadcast_to(jnp.max(best, axis=1, keepdims=True), (8, 128))

def hist_and_best(bins, stats):
    nodes, feats, slots = bins.shape
    st = stats.shape[1]
    hist, best = pl.pallas_call(
        histogram_kernel, grid=(nodes,),
        in_specs=[pl.BlockSpec((1, feats, slots), lambda n: (n, 0, 0)),
                  pl.BlockSpec((1, st, slots), lambda n: (n, 0, 0))],
        out_specs=[pl.BlockSpec((1, feats, st, B), lambda n: (n, 0, 0, 0)),
                   pl.BlockSpec((1, 8, 128), lambda n: (n, 0, 0))],
        out_shape=[jax.ShapeDtypeStruct((nodes, feats, st, B), jnp.float32),
                   jax.ShapeDtypeStruct((nodes, 8, 128), jnp.float32)])(bins, stats)
    return hist, best[:, 0, 0]

def running_rank(owned):
    rows, nodes = owned.shape
    blocks = rows // BLOCK
    ob = owned.reshape(blocks, BLOCK, nodes).astype(jnp.bfloat16)
    i = lax.broadcasted_iota(jnp.int32, (BLOCK, BLOCK), 0)
    j = lax.broadcasted_iota(jnp.int32, (BLOCK, BLOCK), 1)
    lower = (i >= j).astype(jnp.bfloat16)
    within = jnp.einsum("ij,bjn->bin", lower, ob, preferred_element_type=jnp.float32)
    totals = within[:, -1, :]
    a = lax.broadcasted_iota(jnp.int32, (blocks, blocks), 0)
    c = lax.broadcasted_iota(jnp.int32, (blocks, blocks), 1)
    before = (a > c).astype(jnp.float32)
    prefix = jnp.einsum("ac,cn->an", before, totals, precision=lax.Precision.HIGHEST)
    counts = within + prefix[:, None, :]
    mine = jnp.sum(counts * ob.astype(jnp.float32), axis=2).reshape(rows)
    return mine.astype(jnp.int32) - 1


def on_device(covariates, pseudo, honest, destination, node_slot):
    feat_count, row_count = covariates.shape
    node_devices = lax.axis_size("node")
    feat_devices = lax.axis_size("feat")
    node_total = node_slot.shape[0]
    node_local = node_total // node_devices
    capacity = 2 * row_count // node_total
    kept = honest == 0
    columns = lax.broadcasted_iota(jnp.int32, (1, node_total), 1)
    named = (destination == columns).astype(jnp.int32)
    target = jnp.sum(named * node_slot[None, :], axis=1)
    owned = ((target[:, None] == columns) & kept[:, None]).astype(jnp.int32)
    rank = running_rank(owned)
    slots = node_total * capacity
    position = jnp.where(kept, target * capacity + rank, slots)
    payload = jnp.concatenate([covariates, pseudo], axis=0)
    payload_width = payload.shape[0]
    empty = jnp.concatenate(
        [jnp.ones((feat_count, slots), jnp.bfloat16), jnp.zeros((payload_width - feat_count, slots), jnp.bfloat16)]
    )
    outgoing = empty.at[:, position].set(payload, mode="drop")
    outgoing = outgoing.reshape(payload_width, node_devices, node_local, capacity)
    arrived = lax.all_to_all(outgoing, "node", split_axis=1, concat_axis=3, tiled=True)[:, 0]
    bin_table = jnp.floor(arrived[:feat_count].astype(jnp.float32) * B).astype(jnp.int32)
    bin_table = jnp.transpose(bin_table, (1, 0, 2))
    ones = jnp.ones((node_local, 1, arrived.shape[2]), jnp.bfloat16)
    statistics = jnp.concatenate([ones, jnp.transpose(arrived[feat_count:], (1, 0, 2))], axis=1)
    histogram, best_local = hist_and_best(bin_table, statistics)
    spread = jnp.broadcast_to(best_local[None, :], (feat_devices, node_local))
    gathered = lax.all_to_all(spread, "feat", split_axis=0, concat_axis=0, tiled=True)
    best_gain = jnp.max(gathered, axis=0)
    return (histogram, best_gain)


def solution(mesh):
    placed = (P("feat", "node"), P(None, "node"), P("node"), P("node", None), P())
    return jax.shard_map(
        on_device,
        mesh=mesh,
        in_specs=placed,
        out_specs=(P("node", "feat", None, None), P("node")),
        check_vma=False,
    )
```

```python
import jax
import jax.numpy as jnp
from jax import lax
from jax.experimental import pallas as pl
from jax.experimental.pallas import tpu as pltpu
from jax.sharding import PartitionSpec as P

B = 256
BLOCK = 256
CH = 512


def histogram_kernel(flags_ref, bins_ref, stats_ref, hist_ref, best_ref):
    feats = bins_ref.shape[1]
    slots = bins_ref.shape[2]
    stat_count = stats_ref.shape[1]
    chunks = slots // CH
    node = pl.program_id(0)
    levels = lax.broadcasted_iota(jnp.int32, (B, CH), 0)
    best = jnp.full((1, B), -jnp.inf, jnp.float32)
    hist_ref[...] = jnp.zeros(hist_ref.shape, hist_ref.dtype)
    for k in range(chunks):

        @pl.when(flags_ref[node * chunks + k] > 0)
        def _():
            for f in range(feats):
                row = bins_ref[0, f:f + 1, k * CH:(k + 1) * CH]
                indicator = (levels == row).astype(jnp.bfloat16)
                hist_ref[0, f] += lax.dot_general(
                    stats_ref[0, :, k * CH:(k + 1) * CH], indicator, (((1,), (1,)), ((), ())),
                    preferred_element_type=jnp.float32)

    lane = lax.broadcasted_iota(jnp.int32, (stat_count, B), 1)
    for f in range(feats):
        left = hist_ref[0, f]
        shift = 1
        while shift < B:
            moved = pltpu.roll(left, shift, 1)
            left = left + jnp.where(lane >= shift, moved, 0.0)
            shift *= 2
        total = left[:, B - 1:B]
        right = total - left
        left_part = jnp.sum(left[1:] * left[1:], axis=0, keepdims=True) / (left[0:1] + 1.0)
        right_part = jnp.sum(right[1:] * right[1:], axis=0, keepdims=True) / (right[0:1] + 1.0)
        total_part = jnp.sum(total[1:] * total[1:], axis=0, keepdims=True) / (total[0:1] + 1.0)
        best = jnp.maximum(best, left_part + right_part - total_part)
    best_ref[0] = jnp.broadcast_to(jnp.max(best, axis=1, keepdims=True), (8, 128))

def hist_and_best(bins, stats):
    nodes, feats, slots = bins.shape
    st = stats.shape[1]
    chunks = slots // CH
    filled = jnp.any(bins[:, 0].reshape(nodes, chunks, CH) < B, axis=2)
    flags = filled.astype(jnp.int32).reshape(nodes * chunks)
    hist, best = pl.pallas_call(
        histogram_kernel,
        grid_spec=pltpu.PrefetchScalarGridSpec(
            num_scalar_prefetch=1,
            grid=(nodes,),
            in_specs=[pl.BlockSpec((1, feats, slots), lambda n, fl: (n, 0, 0)),
                      pl.BlockSpec((1, st, slots), lambda n, fl: (n, 0, 0))],
            out_specs=[pl.BlockSpec((1, feats, st, B), lambda n, fl: (n, 0, 0, 0)),
                       pl.BlockSpec((1, 8, 128), lambda n, fl: (n, 0, 0))]),
        out_shape=[jax.ShapeDtypeStruct((nodes, feats, st, B), jnp.float32),
                   jax.ShapeDtypeStruct((nodes, 8, 128), jnp.float32)])(flags, bins, stats)
    return hist, best[:, 0, 0]


def running_rank(owned):
    rows, nodes = owned.shape
    blocks = rows // BLOCK
    ob = owned.reshape(blocks, BLOCK, nodes).astype(jnp.bfloat16)
    i = lax.broadcasted_iota(jnp.int32, (BLOCK, BLOCK), 0)
    j = lax.broadcasted_iota(jnp.int32, (BLOCK, BLOCK), 1)
    lower = (i >= j).astype(jnp.bfloat16)
    within = jnp.einsum("ij,bjn->bin", lower, ob, preferred_element_type=jnp.float32)
    totals = within[:, -1, :]
    a = lax.broadcasted_iota(jnp.int32, (blocks, blocks), 0)
    c = lax.broadcasted_iota(jnp.int32, (blocks, blocks), 1)
    before = (a > c).astype(jnp.float32)
    prefix = jnp.einsum("ac,cn->an", before, totals, precision=lax.Precision.HIGHEST)
    counts = within + prefix[:, None, :]
    mine = jnp.sum(counts * ob.astype(jnp.float32), axis=2).reshape(rows)
    return mine.astype(jnp.int32) - 1


def on_device(covariates, pseudo, honest, destination, node_slot):
    feat_count, row_count = covariates.shape
    node_devices = lax.axis_size("node")
    feat_devices = lax.axis_size("feat")
    node_total = node_slot.shape[0]
    node_local = node_total // node_devices
    capacity = 2 * row_count // node_total
    kept = honest == 0
    columns = lax.broadcasted_iota(jnp.int32, (1, node_total), 1)
    named = (destination == columns).astype(jnp.int32)
    target = jnp.sum(named * node_slot[None, :], axis=1)
    owned = ((target[:, None] == columns) & kept[:, None]).astype(jnp.int32)
    rank = running_rank(owned)
    slots = node_total * capacity
    position = jnp.where(kept, target * capacity + rank, slots)
    payload = jnp.concatenate([covariates, pseudo], axis=0)
    payload_width = payload.shape[0]
    empty = jnp.concatenate(
        [jnp.ones((feat_count, slots), jnp.bfloat16), jnp.zeros((payload_width - feat_count, slots), jnp.bfloat16)]
    )
    outgoing = empty.at[:, position].set(payload, mode="drop")
    outgoing = outgoing.reshape(payload_width, node_devices, node_local, capacity)
    arrived = lax.all_to_all(outgoing, "node", split_axis=1, concat_axis=3, tiled=True)[:, 0]
    arrived = arrived.reshape(payload_width, node_local, node_devices, capacity)
    arrived = jnp.transpose(arrived, (0, 1, 3, 2)).reshape(payload_width, node_local, node_devices * capacity)
    bin_table = jnp.floor(arrived[:feat_count].astype(jnp.float32) * B).astype(jnp.int32)
    bin_table = jnp.transpose(bin_table, (1, 0, 2))
    ones = jnp.ones((node_local, 1, arrived.shape[2]), jnp.bfloat16)
    statistics = jnp.concatenate([ones, jnp.transpose(arrived[feat_count:], (1, 0, 2))], axis=1)
    histogram, best_local = hist_and_best(bin_table, statistics)
    spread = jnp.broadcast_to(best_local[None, :], (feat_devices, node_local))
    gathered = lax.all_to_all(spread, "feat", split_axis=0, concat_axis=0, tiled=True)
    best_gain = jnp.max(gathered, axis=0)
    return (histogram, best_gain)


def solution(mesh):
    placed = (P("feat", "node"), P(None, "node"), P("node"), P("node", None), P())
    return jax.shard_map(
        on_device,
        mesh=mesh,
        in_specs=placed,
        out_specs=(P("node", "feat", None, None), P("node")),
        check_vma=False,
    )
```

```python
import jax
import jax.numpy as jnp
from jax import lax
from jax.experimental import pallas as pl
from jax.experimental.pallas import tpu as pltpu
from jax.sharding import PartitionSpec as P

B = 256
BLOCK = 256
CH = 512


def histogram_kernel(flags_ref, bins_ref, stats_ref, hist_ref, best_ref):
    feats = bins_ref.shape[1]
    slots = bins_ref.shape[2]
    stat_count = stats_ref.shape[1]
    chunks = slots // CH
    node = pl.program_id(0)
    levels = lax.broadcasted_iota(jnp.int32, (B, CH), 0)
    best = jnp.full((1, B), -jnp.inf, jnp.float32)
    hist_ref[...] = jnp.zeros(hist_ref.shape, hist_ref.dtype)
    for k in range(chunks):

        @pl.when(flags_ref[node * chunks + k] > 0)
        def _():
            for f in range(feats):
                row = bins_ref[0, f:f + 1, k * CH:(k + 1) * CH]
                indicator = (levels == row).astype(jnp.bfloat16)
                hist_ref[0, f] += lax.dot_general(
                    stats_ref[0, :, k * CH:(k + 1) * CH], indicator, (((1,), (1,)), ((), ())),
                    preferred_element_type=jnp.float32)

    lane = lax.broadcasted_iota(jnp.int32, (stat_count, B), 1)
    for f in range(feats):
        left = hist_ref[0, f]
        shift = 1
        while shift < B:
            moved = pltpu.roll(left, shift, 1)
            left = left + jnp.where(lane >= shift, moved, 0.0)
            shift *= 2
        total = left[:, B - 1:B]
        right = total - left
        left_part = jnp.sum(left[1:] * left[1:], axis=0, keepdims=True) / (left[0:1] + 1.0)
        right_part = jnp.sum(right[1:] * right[1:], axis=0, keepdims=True) / (right[0:1] + 1.0)
        total_part = jnp.sum(total[1:] * total[1:], axis=0, keepdims=True) / (total[0:1] + 1.0)
        best = jnp.maximum(best, left_part + right_part - total_part)
    best_ref[0] = jnp.broadcast_to(jnp.max(best, axis=1, keepdims=True), (8, 128))

def hist_and_best(bins, stats):
    nodes, feats, slots = bins.shape
    st = stats.shape[1]
    chunks = slots // CH
    filled = jnp.any(bins[:, 0].reshape(nodes, chunks, CH) < B, axis=2)
    flags = filled.astype(jnp.int32).reshape(nodes * chunks)
    hist, best = pl.pallas_call(
        histogram_kernel,
        grid_spec=pltpu.PrefetchScalarGridSpec(
            num_scalar_prefetch=1,
            grid=(nodes,),
            in_specs=[pl.BlockSpec((1, feats, slots), lambda n, fl: (n, 0, 0)),
                      pl.BlockSpec((1, st, slots), lambda n, fl: (n, 0, 0))],
            out_specs=[pl.BlockSpec((1, feats, st, B), lambda n, fl: (n, 0, 0, 0)),
                       pl.BlockSpec((1, 8, 128), lambda n, fl: (n, 0, 0))]),
        out_shape=[jax.ShapeDtypeStruct((nodes, feats, st, B), jnp.float32),
                   jax.ShapeDtypeStruct((nodes, 8, 128), jnp.float32)])(flags, bins, stats)
    return hist, best[:, 0, 0]


def running_rank(owned):
    rows, nodes = owned.shape
    blocks = rows // BLOCK
    ob = owned.reshape(blocks, BLOCK, nodes).astype(jnp.bfloat16)
    i = lax.broadcasted_iota(jnp.int32, (BLOCK, BLOCK), 0)
    j = lax.broadcasted_iota(jnp.int32, (BLOCK, BLOCK), 1)
    lower = (i >= j).astype(jnp.bfloat16)
    within = jnp.einsum("ij,bjn->bin", lower, ob, preferred_element_type=jnp.float32)
    totals = within[:, -1, :]
    a = lax.broadcasted_iota(jnp.int32, (blocks, blocks), 0)
    c = lax.broadcasted_iota(jnp.int32, (blocks, blocks), 1)
    before = (a > c).astype(jnp.float32)
    prefix = jnp.einsum("ac,cn->an", before, totals, precision=lax.Precision.HIGHEST)
    counts = within + prefix[:, None, :]
    mine = jnp.sum(counts * ob.astype(jnp.float32), axis=2).reshape(rows)
    return mine.astype(jnp.int32) - 1


def on_device(covariates, pseudo, honest, destination, node_slot):
    feat_count, row_count = covariates.shape
    node_devices = lax.axis_size("node")
    feat_devices = lax.axis_size("feat")
    node_total = node_slot.shape[0]
    node_local = node_total // node_devices
    capacity = 2 * row_count // node_total
    kept = honest == 0
    columns = lax.broadcasted_iota(jnp.int32, (1, node_total), 1)
    named = (destination == columns).astype(jnp.int32)
    target = jnp.sum(named * node_slot[None, :], axis=1)
    owned = ((target[:, None] == columns) & kept[:, None]).astype(jnp.int32)
    rank = running_rank(owned)
    slots = node_total * capacity
    position = jnp.where(kept, target * capacity + rank, slots)
    payload = jnp.concatenate([covariates, pseudo], axis=0)
    payload_width = payload.shape[0]
    empty = jnp.concatenate(
        [jnp.ones((feat_count, slots), jnp.bfloat16), jnp.zeros((payload_width - feat_count, slots), jnp.bfloat16)]
    )
    outgoing = empty.T.at[position].set(payload.T, mode="drop")
    outgoing = outgoing.reshape(node_devices, node_local * capacity, payload_width)
    arrived = lax.all_to_all(outgoing, "node", split_axis=0, concat_axis=0, tiled=True)
    arrived = arrived.reshape(node_devices, node_local, capacity, payload_width)
    arrived = jnp.transpose(arrived, (3, 1, 2, 0)).reshape(payload_width, node_local, capacity * node_devices)
    bin_table = jnp.floor(arrived[:feat_count].astype(jnp.float32) * B).astype(jnp.int32)
    bin_table = jnp.transpose(bin_table, (1, 0, 2))
    ones = jnp.ones((node_local, 1, arrived.shape[2]), jnp.bfloat16)
    statistics = jnp.concatenate([ones, jnp.transpose(arrived[feat_count:], (1, 0, 2))], axis=1)
    histogram, best_local = hist_and_best(bin_table, statistics)
    spread = jnp.broadcast_to(best_local[None, :], (feat_devices, node_local))
    gathered = lax.all_to_all(spread, "feat", split_axis=0, concat_axis=0, tiled=True)
    best_gain = jnp.max(gathered, axis=0)
    return (histogram, best_gain)


def solution(mesh):
    placed = (P("feat", "node"), P(None, "node"), P("node"), P("node", None), P())
    return jax.shard_map(
        on_device,
        mesh=mesh,
        in_specs=placed,
        out_specs=(P("node", "feat", None, None), P("node")),
        check_vma=False,
    )
```

```python
import jax
import jax.numpy as jnp
from jax import lax
from jax.experimental import pallas as pl
from jax.experimental.pallas import tpu as pltpu
from jax.sharding import PartitionSpec as P

B = 256
BLOCK = 256
CH = 512


def histogram_kernel(flags_ref, rows_ref, hist_ref, best_ref):
    feats = hist_ref.shape[1]
    stat_count = hist_ref.shape[2]
    slots = rows_ref.shape[2]
    chunks = slots // CH
    node = pl.program_id(0)
    levels = lax.broadcasted_iota(jnp.int32, (B, CH), 0).astype(jnp.float32)
    best = jnp.full((1, B), -jnp.inf, jnp.float32)
    hist_ref[...] = jnp.zeros(hist_ref.shape, hist_ref.dtype)
    for k in range(chunks):

        @pl.when(flags_ref[node * chunks + k] > 0)
        def _():
            stats = rows_ref[0, feats:feats + stat_count, k * CH:(k + 1) * CH]
            for f in range(feats):
                row = rows_ref[0, f:f + 1, k * CH:(k + 1) * CH]
                bins = jnp.floor(row.astype(jnp.float32) * B)
                indicator = (levels == bins).astype(jnp.bfloat16)
                hist_ref[0, f] += lax.dot_general(
                    stats, indicator, (((1,), (1,)), ((), ())), preferred_element_type=jnp.float32)

    lane = lax.broadcasted_iota(jnp.int32, (stat_count, B), 1)
    for f in range(feats):
        left = hist_ref[0, f]
        shift = 1
        while shift < B:
            moved = pltpu.roll(left, shift, 1)
            left = left + jnp.where(lane >= shift, moved, 0.0)
            shift *= 2
        total = left[:, B - 1:B]
        right = total - left
        left_part = jnp.sum(left[1:] * left[1:], axis=0, keepdims=True) / (left[0:1] + 1.0)
        right_part = jnp.sum(right[1:] * right[1:], axis=0, keepdims=True) / (right[0:1] + 1.0)
        total_part = jnp.sum(total[1:] * total[1:], axis=0, keepdims=True) / (total[0:1] + 1.0)
        best = jnp.maximum(best, left_part + right_part - total_part)
    best_ref[0] = jnp.broadcast_to(jnp.max(best, axis=1, keepdims=True), (8, 128))

def hist_and_best(rows, feats):
    nodes, width, slots = rows.shape
    st = width - feats
    chunks = slots // CH
    filled = jnp.any(rows[:, 0].reshape(nodes, chunks, CH) < 1.0, axis=2)
    flags = filled.astype(jnp.int32).reshape(nodes * chunks)
    hist, best = pl.pallas_call(
        histogram_kernel,
        grid_spec=pltpu.PrefetchScalarGridSpec(
            num_scalar_prefetch=1,
            grid=(nodes,),
            in_specs=[pl.BlockSpec((1, width, slots), lambda n, fl: (n, 0, 0))],
            out_specs=[pl.BlockSpec((1, feats, st, B), lambda n, fl: (n, 0, 0, 0)),
                       pl.BlockSpec((1, 8, 128), lambda n, fl: (n, 0, 0))]),
        out_shape=[jax.ShapeDtypeStruct((nodes, feats, st, B), jnp.float32),
                   jax.ShapeDtypeStruct((nodes, 8, 128), jnp.float32)])(flags, rows)
    return hist, best[:, 0, 0]


def running_rank(owned):
    rows, nodes = owned.shape
    blocks = rows // BLOCK
    ob = owned.reshape(blocks, BLOCK, nodes).astype(jnp.bfloat16)
    i = lax.broadcasted_iota(jnp.int32, (BLOCK, BLOCK), 0)
    j = lax.broadcasted_iota(jnp.int32, (BLOCK, BLOCK), 1)
    lower = (i >= j).astype(jnp.bfloat16)
    within = jnp.einsum("ij,bjn->bin", lower, ob, preferred_element_type=jnp.float32)
    totals = within[:, -1, :]
    a = lax.broadcasted_iota(jnp.int32, (blocks, blocks), 0)
    c = lax.broadcasted_iota(jnp.int32, (blocks, blocks), 1)
    before = (a > c).astype(jnp.float32)
    prefix = jnp.einsum("ac,cn->an", before, totals, precision=lax.Precision.HIGHEST)
    counts = within + prefix[:, None, :]
    mine = jnp.sum(counts * ob.astype(jnp.float32), axis=2).reshape(rows)
    return mine.astype(jnp.int32) - 1


def on_device(covariates, pseudo, honest, destination, node_slot):
    feat_count, row_count = covariates.shape
    node_devices = lax.axis_size("node")
    feat_devices = lax.axis_size("feat")
    node_total = node_slot.shape[0]
    node_local = node_total // node_devices
    capacity = 2 * row_count // node_total
    kept = honest == 0
    columns = lax.broadcasted_iota(jnp.int32, (1, node_total), 1)
    named = (destination == columns).astype(jnp.int32)
    target = jnp.sum(named * node_slot[None, :], axis=1)
    owned = ((target[:, None] == columns) & kept[:, None]).astype(jnp.int32)
    rank = running_rank(owned)
    slots = node_total * capacity
    position = jnp.where(kept, target * capacity + rank, slots)
    weight_row = jnp.ones((1, row_count), jnp.bfloat16)
    payload = jnp.concatenate([covariates, weight_row, pseudo], axis=0)
    payload_width = payload.shape[0]
    empty = jnp.concatenate(
        [jnp.ones((feat_count, slots), jnp.bfloat16), jnp.zeros((payload_width - feat_count, slots), jnp.bfloat16)]
    )
    outgoing = empty.T.at[position].set(payload.T, mode="drop")
    outgoing = outgoing.reshape(node_devices, node_local * capacity, payload_width)
    arrived = lax.all_to_all(outgoing, "node", split_axis=0, concat_axis=0, tiled=True)
    arrived = arrived.reshape(node_devices, node_local, capacity, payload_width)
    rows = jnp.transpose(arrived, (1, 3, 2, 0)).reshape(node_local, payload_width, capacity * node_devices)
    histogram, best_local = hist_and_best(rows, feat_count)
    spread = jnp.broadcast_to(best_local[None, :], (feat_devices, node_local))
    gathered = lax.all_to_all(spread, "feat", split_axis=0, concat_axis=0, tiled=True)
    best_gain = jnp.max(gathered, axis=0)
    return (histogram, best_gain)


def solution(mesh):
    placed = (P("feat", "node"), P(None, "node"), P("node"), P("node", None), P())
    return jax.shard_map(
        on_device,
        mesh=mesh,
        in_specs=placed,
        out_specs=(P("node", "feat", None, None), P("node")),
        check_vma=False,
    )
```

```python
import jax
import jax.numpy as jnp
from jax import lax
from jax.experimental import pallas as pl
from jax.experimental.pallas import tpu as pltpu
from jax.sharding import PartitionSpec as P

B = 256
BLOCK = 256
CH = 256


def histogram_kernel(flags_ref, bins_ref, stats_ref, hist_ref, best_ref):
    feats = bins_ref.shape[1]
    slots = bins_ref.shape[2]
    stat_count = stats_ref.shape[1]
    chunks = slots // CH
    node = pl.program_id(0)
    levels = lax.broadcasted_iota(jnp.int32, (B, CH), 0)
    best = jnp.full((1, B), -jnp.inf, jnp.float32)
    hist_ref[...] = jnp.zeros(hist_ref.shape, hist_ref.dtype)
    for k in range(chunks):

        @pl.when(flags_ref[node * chunks + k] > 0)
        def _():
            for f in range(feats):
                row = bins_ref[0, f:f + 1, k * CH:(k + 1) * CH]
                indicator = (levels == row).astype(jnp.bfloat16)
                hist_ref[0, f] += lax.dot_general(
                    stats_ref[0, :, k * CH:(k + 1) * CH], indicator, (((1,), (1,)), ((), ())),
                    preferred_element_type=jnp.float32)

    lane = lax.broadcasted_iota(jnp.int32, (stat_count, B), 1)
    for f in range(feats):
        left = hist_ref[0, f]
        shift = 1
        while shift < B:
            moved = pltpu.roll(left, shift, 1)
            left = left + jnp.where(lane >= shift, moved, 0.0)
            shift *= 2
        total = left[:, B - 1:B]
        right = total - left
        left_part = jnp.sum(left[1:] * left[1:], axis=0, keepdims=True) / (left[0:1] + 1.0)
        right_part = jnp.sum(right[1:] * right[1:], axis=0, keepdims=True) / (right[0:1] + 1.0)
        total_part = jnp.sum(total[1:] * total[1:], axis=0, keepdims=True) / (total[0:1] + 1.0)
        best = jnp.maximum(best, left_part + right_part - total_part)
    best_ref[0] = jnp.broadcast_to(jnp.max(best, axis=1, keepdims=True), (8, 128))

def hist_and_best(bins, stats):
    nodes, feats, slots = bins.shape
    st = stats.shape[1]
    chunks = slots // CH
    filled = jnp.any(bins[:, 0].reshape(nodes, chunks, CH) < B, axis=2)
    flags = filled.astype(jnp.int32).reshape(nodes * chunks)
    hist, best = pl.pallas_call(
        histogram_kernel,
        grid_spec=pltpu.PrefetchScalarGridSpec(
            num_scalar_prefetch=1,
            grid=(nodes,),
            in_specs=[pl.BlockSpec((1, feats, slots), lambda n, fl: (n, 0, 0)),
                      pl.BlockSpec((1, st, slots), lambda n, fl: (n, 0, 0))],
            out_specs=[pl.BlockSpec((1, feats, st, B), lambda n, fl: (n, 0, 0, 0)),
                       pl.BlockSpec((1, 8, 128), lambda n, fl: (n, 0, 0))]),
        out_shape=[jax.ShapeDtypeStruct((nodes, feats, st, B), jnp.float32),
                   jax.ShapeDtypeStruct((nodes, 8, 128), jnp.float32)])(flags, bins, stats)
    return hist, best[:, 0, 0]


def running_rank(owned):
    rows, nodes = owned.shape
    blocks = rows // BLOCK
    ob = owned.reshape(blocks, BLOCK, nodes).astype(jnp.bfloat16)
    i = lax.broadcasted_iota(jnp.int32, (BLOCK, BLOCK), 0)
    j = lax.broadcasted_iota(jnp.int32, (BLOCK, BLOCK), 1)
    lower = (i >= j).astype(jnp.bfloat16)
    within = jnp.einsum("ij,bjn->bin", lower, ob, preferred_element_type=jnp.float32)
    totals = within[:, -1, :]
    a = lax.broadcasted_iota(jnp.int32, (blocks, blocks), 0)
    c = lax.broadcasted_iota(jnp.int32, (blocks, blocks), 1)
    before = (a > c).astype(jnp.float32)
    prefix = jnp.einsum("ac,cn->an", before, totals, precision=lax.Precision.HIGHEST)
    counts = within + prefix[:, None, :]
    mine = jnp.sum(counts * ob.astype(jnp.float32), axis=2).reshape(rows)
    return mine.astype(jnp.int32) - 1


def on_device(covariates, pseudo, honest, destination, node_slot):
    feat_count, row_count = covariates.shape
    node_devices = lax.axis_size("node")
    feat_devices = lax.axis_size("feat")
    node_total = node_slot.shape[0]
    node_local = node_total // node_devices
    capacity = 2 * row_count // node_total
    kept = honest == 0
    columns = lax.broadcasted_iota(jnp.int32, (1, node_total), 1)
    named = (destination == columns).astype(jnp.int32)
    target = jnp.sum(named * node_slot[None, :], axis=1)
    owned = ((target[:, None] == columns) & kept[:, None]).astype(jnp.int32)
    rank = running_rank(owned)
    slots = node_total * capacity
    position = jnp.where(kept, target * capacity + rank, slots)
    payload = jnp.concatenate([covariates, pseudo], axis=0)
    payload_width = payload.shape[0]
    empty = jnp.concatenate(
        [jnp.ones((feat_count, slots), jnp.bfloat16), jnp.zeros((payload_width - feat_count, slots), jnp.bfloat16)]
    )
    outgoing = empty.T.at[position].set(payload.T, mode="drop")
    outgoing = outgoing.reshape(node_devices, node_local * capacity, payload_width)
    arrived = lax.all_to_all(outgoing, "node", split_axis=0, concat_axis=0, tiled=True)
    arrived = arrived.reshape(node_devices, node_local, capacity, payload_width)
    arrived = jnp.transpose(arrived, (3, 1, 2, 0)).reshape(payload_width, node_local, capacity * node_devices)
    bin_table = jnp.floor(arrived[:feat_count].astype(jnp.float32) * B).astype(jnp.int32)
    bin_table = jnp.transpose(bin_table, (1, 0, 2))
    ones = jnp.ones((node_local, 1, arrived.shape[2]), jnp.bfloat16)
    statistics = jnp.concatenate([ones, jnp.transpose(arrived[feat_count:], (1, 0, 2))], axis=1)
    histogram, best_local = hist_and_best(bin_table, statistics)
    spread = jnp.broadcast_to(best_local[None, :], (feat_devices, node_local))
    gathered = lax.all_to_all(spread, "feat", split_axis=0, concat_axis=0, tiled=True)
    best_gain = jnp.max(gathered, axis=0)
    return (histogram, best_gain)


def solution(mesh):
    placed = (P("feat", "node"), P(None, "node"), P("node"), P("node", None), P())
    return jax.shard_map(
        on_device,
        mesh=mesh,
        in_specs=placed,
        out_specs=(P("node", "feat", None, None), P("node")),
        check_vma=False,
    )
```

```python
import jax
import jax.numpy as jnp
from jax import lax
from jax.experimental import pallas as pl
from jax.experimental.pallas import tpu as pltpu
from jax.sharding import PartitionSpec as P

B = 256
BLOCK = 256
CH = 128
GROUPS = 4


def histogram_kernel(flags_ref, bins_ref, stats_ref, hist_ref, best_ref):
    feats = bins_ref.shape[1]
    slots = bins_ref.shape[2]
    stat_count = stats_ref.shape[1]
    chunks = slots // CH
    node = pl.program_id(0)
    levels = lax.broadcasted_iota(jnp.int32, (B, CH), 0)
    best = jnp.full((1, B), -jnp.inf, jnp.float32)
    hist_ref[...] = jnp.zeros(hist_ref.shape, hist_ref.dtype)
    def chunk(k, carry):
        @pl.when(flags_ref[node * chunks + k] > 0)
        def _():
            offset = pl.multiple_of(k * CH, CH)
            stats = stats_ref[0, :, pl.ds(offset, CH)]
            for f in range(feats):
                row = bins_ref[0, f:f + 1, pl.ds(offset, CH)]
                indicator = (levels == row).astype(jnp.bfloat16)
                hist_ref[0, f] += lax.dot_general(
                    stats, indicator, (((1,), (1,)), ((), ())), preferred_element_type=jnp.float32)

        return carry

    lax.fori_loop(0, chunks, chunk, 0)
    lane = lax.broadcasted_iota(jnp.int32, (stat_count, B), 1)
    for f in range(feats):
        left = hist_ref[0, f]
        shift = 1
        while shift < B:
            moved = pltpu.roll(left, shift, 1)
            left = left + jnp.where(lane >= shift, moved, 0.0)
            shift *= 2
        total = left[:, B - 1:B]
        right = total - left
        left_part = jnp.sum(left[1:] * left[1:], axis=0, keepdims=True) / (left[0:1] + 1.0)
        right_part = jnp.sum(right[1:] * right[1:], axis=0, keepdims=True) / (right[0:1] + 1.0)
        total_part = jnp.sum(total[1:] * total[1:], axis=0, keepdims=True) / (total[0:1] + 1.0)
        best = jnp.maximum(best, left_part + right_part - total_part)
    best_ref[0] = jnp.broadcast_to(jnp.max(best, axis=1, keepdims=True), (8, 128))

def hist_and_best(bins, stats):
    nodes, feats, slots = bins.shape
    st = stats.shape[1]
    chunks = slots // CH
    filled = jnp.any(bins[:, 0].reshape(nodes, chunks, CH) < B, axis=2)
    flags = filled.astype(jnp.int32).reshape(nodes * chunks)
    hist, best = pl.pallas_call(
        histogram_kernel,
        grid_spec=pltpu.PrefetchScalarGridSpec(
            num_scalar_prefetch=1,
            grid=(nodes,),
            in_specs=[pl.BlockSpec((1, feats, slots), lambda n, fl: (n, 0, 0)),
                      pl.BlockSpec((1, st, slots), lambda n, fl: (n, 0, 0))],
            out_specs=[pl.BlockSpec((1, feats, st, B), lambda n, fl: (n, 0, 0, 0)),
                       pl.BlockSpec((1, 8, 128), lambda n, fl: (n, 0, 0))]),
        out_shape=[jax.ShapeDtypeStruct((nodes, feats, st, B), jnp.float32),
                   jax.ShapeDtypeStruct((nodes, 8, 128), jnp.float32)])(flags, bins, stats)
    return hist, best[:, 0, 0]


def running_rank(owned):
    rows, nodes = owned.shape
    blocks = rows // BLOCK
    ob = owned.reshape(blocks, BLOCK, nodes).astype(jnp.bfloat16)
    i = lax.broadcasted_iota(jnp.int32, (BLOCK, BLOCK), 0)
    j = lax.broadcasted_iota(jnp.int32, (BLOCK, BLOCK), 1)
    lower = (i >= j).astype(jnp.bfloat16)
    within = jnp.einsum("ij,bjn->bin", lower, ob, preferred_element_type=jnp.float32)
    totals = within[:, -1, :]
    a = lax.broadcasted_iota(jnp.int32, (blocks, blocks), 0)
    c = lax.broadcasted_iota(jnp.int32, (blocks, blocks), 1)
    before = (a > c).astype(jnp.float32)
    prefix = jnp.einsum("ac,cn->an", before, totals, precision=lax.Precision.HIGHEST)
    counts = within + prefix[:, None, :]
    mine = jnp.sum(counts * ob.astype(jnp.float32), axis=2).reshape(rows)
    return mine.astype(jnp.int32) - 1


def on_device(covariates, pseudo, honest, destination, node_slot):
    feat_count, row_count = covariates.shape
    node_devices = lax.axis_size("node")
    feat_devices = lax.axis_size("feat")
    node_total = node_slot.shape[0]
    node_local = node_total // node_devices
    capacity = 2 * row_count // node_total
    kept = honest == 0
    columns = lax.broadcasted_iota(jnp.int32, (1, node_total), 1)
    named = (destination == columns).astype(jnp.int32)
    target = jnp.sum(named * node_slot[None, :], axis=1)
    owned = ((target[:, None] == columns) & kept[:, None]).astype(jnp.int32)
    rank = running_rank(owned)
    slots = node_total * capacity
    position = jnp.where(kept, target * capacity + rank, slots)
    payload = jnp.concatenate([covariates, pseudo], axis=0)
    payload_width = payload.shape[0]
    empty = jnp.concatenate(
        [jnp.ones((feat_count, slots), jnp.bfloat16), jnp.zeros((payload_width - feat_count, slots), jnp.bfloat16)]
    )
    outgoing = empty.T.at[position].set(payload.T, mode="drop")
    outgoing = outgoing.reshape(node_devices, node_local * capacity, payload_width)
    arrived = lax.all_to_all(outgoing, "node", split_axis=0, concat_axis=0, tiled=True)
    arrived = arrived.reshape(GROUPS, node_devices // GROUPS, node_local, capacity, payload_width)
    arrived = jnp.transpose(arrived, (4, 2, 0, 3, 1)).reshape(payload_width, node_local, capacity * node_devices)
    bin_table = jnp.floor(arrived[:feat_count].astype(jnp.float32) * B).astype(jnp.int32)
    bin_table = jnp.transpose(bin_table, (1, 0, 2))
    ones = jnp.ones((node_local, 1, arrived.shape[2]), jnp.bfloat16)
    statistics = jnp.concatenate([ones, jnp.transpose(arrived[feat_count:], (1, 0, 2))], axis=1)
    histogram, best_local = hist_and_best(bin_table, statistics)
    spread = jnp.broadcast_to(best_local[None, :], (feat_devices, node_local))
    gathered = lax.all_to_all(spread, "feat", split_axis=0, concat_axis=0, tiled=True)
    best_gain = jnp.max(gathered, axis=0)
    return (histogram, best_gain)


def solution(mesh):
    placed = (P("feat", "node"), P(None, "node"), P("node"), P("node", None), P())
    return jax.shard_map(
        on_device,
        mesh=mesh,
        in_specs=placed,
        out_specs=(P("node", "feat", None, None), P("node")),
        check_vma=False,
    )
```

```python
import jax
import jax.numpy as jnp
from jax import lax
from jax.experimental import pallas as pl
from jax.experimental.pallas import tpu as pltpu
from jax.sharding import PartitionSpec as P

B = 256
BLOCK = 256
CH = 256


def histogram_kernel(flags_ref, bins_ref, stats_ref, hist_ref, best_ref):
    feats = bins_ref.shape[1]
    slots = bins_ref.shape[2]
    stat_count = stats_ref.shape[1]
    chunks = slots // CH
    node = pl.program_id(0)
    levels = lax.broadcasted_iota(jnp.int32, (B, CH), 0).astype(jnp.float32)
    best = jnp.full((1, B), -jnp.inf, jnp.float32)
    hist_ref[...] = jnp.zeros(hist_ref.shape, hist_ref.dtype)
    for k in range(chunks):

        @pl.when(flags_ref[node * chunks + k] > 0)
        def _():
            for f in range(feats):
                row = bins_ref[0, f:f + 1, k * CH:(k + 1) * CH].astype(jnp.float32)
                indicator = (levels == row).astype(jnp.bfloat16)
                hist_ref[0, f] += lax.dot_general(
                    stats_ref[0, :, k * CH:(k + 1) * CH], indicator, (((1,), (1,)), ((), ())),
                    preferred_element_type=jnp.float32)

    lane = lax.broadcasted_iota(jnp.int32, (stat_count, B), 1)
    for f in range(feats):
        left = hist_ref[0, f]
        shift = 1
        while shift < B:
            moved = pltpu.roll(left, shift, 1)
            left = left + jnp.where(lane >= shift, moved, 0.0)
            shift *= 2
        total = left[:, B - 1:B]
        right = total - left
        left_part = jnp.sum(left[1:] * left[1:], axis=0, keepdims=True) / (left[0:1] + 1.0)
        right_part = jnp.sum(right[1:] * right[1:], axis=0, keepdims=True) / (right[0:1] + 1.0)
        total_part = jnp.sum(total[1:] * total[1:], axis=0, keepdims=True) / (total[0:1] + 1.0)
        best = jnp.maximum(best, left_part + right_part - total_part)
    best_ref[0] = jnp.broadcast_to(jnp.max(best, axis=1, keepdims=True), best_ref.shape[1:])

def hist_and_best(bins, stats, spread):
    nodes, feats, slots = bins.shape
    st = stats.shape[1]
    chunks = slots // CH
    filled = jnp.any(bins[:, 0].reshape(nodes, chunks, CH) < B, axis=2)
    flags = filled.astype(jnp.int32).reshape(nodes * chunks)
    hist, best = pl.pallas_call(
        histogram_kernel,
        grid_spec=pltpu.PrefetchScalarGridSpec(
            num_scalar_prefetch=1,
            grid=(nodes,),
            in_specs=[pl.BlockSpec((1, feats, slots), lambda n, fl: (n, 0, 0)),
                      pl.BlockSpec((1, st, slots), lambda n, fl: (n, 0, 0))],
            out_specs=[pl.BlockSpec((1, feats, st, B), lambda n, fl: (n, 0, 0, 0)),
                       pl.BlockSpec((1, spread, 128), lambda n, fl: (n, 0, 0))]),
        out_shape=[jax.ShapeDtypeStruct((nodes, feats, st, B), jnp.float32),
                   jax.ShapeDtypeStruct((nodes, spread, 128), jnp.float32)])(flags, bins, stats)
    return hist, best


def running_rank(owned):
    rows, nodes = owned.shape
    blocks = rows // BLOCK
    ob = owned.reshape(blocks, BLOCK, nodes).astype(jnp.bfloat16)
    i = lax.broadcasted_iota(jnp.int32, (BLOCK, BLOCK), 0)
    j = lax.broadcasted_iota(jnp.int32, (BLOCK, BLOCK), 1)
    lower = (i >= j).astype(jnp.bfloat16)
    within = jnp.einsum("ij,bjn->bin", lower, ob, preferred_element_type=jnp.float32)
    totals = within[:, -1, :]
    a = lax.broadcasted_iota(jnp.int32, (blocks, blocks), 0)
    c = lax.broadcasted_iota(jnp.int32, (blocks, blocks), 1)
    before = (a > c).astype(jnp.float32)
    prefix = jnp.einsum("ac,cn->an", before, totals, precision=lax.Precision.HIGHEST)
    counts = within + prefix[:, None, :]
    mine = jnp.sum(counts * ob.astype(jnp.float32), axis=2).reshape(rows)
    return mine.astype(jnp.int32) - 1


def on_device(covariates, pseudo, honest, destination, node_slot):
    feat_count, row_count = covariates.shape
    node_devices = lax.axis_size("node")
    feat_devices = lax.axis_size("feat")
    node_total = node_slot.shape[0]
    node_local = node_total // node_devices
    capacity = 2 * row_count // node_total
    kept = honest == 0
    columns = lax.broadcasted_iota(jnp.int32, (1, node_total), 1)
    named = (destination == columns).astype(jnp.int32)
    target = jnp.sum(named * node_slot[None, :], axis=1)
    owned = ((target[:, None] == columns) & kept[:, None]).astype(jnp.int32)
    rank = running_rank(owned)
    slots = node_total * capacity
    position = jnp.where(kept, target * capacity + rank, slots)
    payload = jnp.concatenate([covariates, pseudo], axis=0)
    payload_width = payload.shape[0]
    empty = jnp.concatenate(
        [jnp.ones((feat_count, slots), jnp.bfloat16), jnp.zeros((payload_width - feat_count, slots), jnp.bfloat16)]
    )
    outgoing = empty.T.at[position].set(payload.T, mode="drop")
    outgoing = outgoing.reshape(node_devices, node_local * capacity, payload_width)
    arrived = lax.all_to_all(outgoing, "node", split_axis=0, concat_axis=0, tiled=True)
    arrived = arrived.reshape(node_devices, node_local, capacity, payload_width)
    arrived = jnp.transpose(arrived, (3, 1, 2, 0)).reshape(payload_width, node_local, capacity * node_devices)
    bin_table = jnp.floor(arrived[:feat_count] * B)
    bin_table = jnp.transpose(bin_table, (1, 0, 2))
    ones = jnp.ones((node_local, 1, arrived.shape[2]), jnp.bfloat16)
    statistics = jnp.concatenate([ones, jnp.transpose(arrived[feat_count:], (1, 0, 2))], axis=1)
    histogram, best_spread = hist_and_best(bin_table, statistics, feat_devices)
    gathered = lax.all_to_all(best_spread, "feat", split_axis=1, concat_axis=1, tiled=True)
    best_gain = jnp.max(gathered[:, :, 0], axis=1)
    return (histogram, best_gain)


def solution(mesh):
    placed = (P("feat", "node"), P(None, "node"), P("node"), P("node", None), P())
    return jax.shard_map(
        on_device,
        mesh=mesh,
        in_specs=placed,
        out_specs=(P("node", "feat", None, None), P("node")),
        check_vma=False,
    )
```

```python
import jax
import jax.numpy as jnp
from jax import lax
from jax.experimental import pallas as pl
from jax.experimental.pallas import tpu as pltpu
from jax.sharding import PartitionSpec as P

B = 256
BLOCK = 256
CH = 256


def histogram_kernel(flags_ref, bins_ref, stats_ref, hist_ref, best_ref):
    feats = bins_ref.shape[1]
    slots = bins_ref.shape[2]
    stat_count = stats_ref.shape[1]
    chunks = slots // CH
    node = pl.program_id(0)
    levels = lax.broadcasted_iota(jnp.int32, (B, CH), 0).astype(jnp.float32)
    best = jnp.full((1, B), -jnp.inf, jnp.float32)
    hist_ref[...] = jnp.zeros(hist_ref.shape, hist_ref.dtype)
    for k in range(chunks):

        @pl.when(flags_ref[node * chunks + k] > 0)
        def _():
            for f in range(feats):
                row = bins_ref[0, f:f + 1, k * CH:(k + 1) * CH].astype(jnp.float32)
                indicator = (levels == row).astype(jnp.bfloat16)
                hist_ref[0, f] += lax.dot_general(
                    stats_ref[0, :, k * CH:(k + 1) * CH], indicator, (((1,), (1,)), ((), ())),
                    preferred_element_type=jnp.float32)

    lane = lax.broadcasted_iota(jnp.int32, (stat_count, B), 1)
    for f in range(feats):
        left = hist_ref[0, f]
        shift = 1
        while shift < B:
            moved = pltpu.roll(left, shift, 1)
            left = left + jnp.where(lane >= shift, moved, 0.0)
            shift *= 2
        total = left[:, B - 1:B]
        right = total - left
        left_part = jnp.sum(left[1:] * left[1:], axis=0, keepdims=True) / (left[0:1] + 1.0)
        right_part = jnp.sum(right[1:] * right[1:], axis=0, keepdims=True) / (right[0:1] + 1.0)
        total_part = jnp.sum(total[1:] * total[1:], axis=0, keepdims=True) / (total[0:1] + 1.0)
        best = jnp.maximum(best, left_part + right_part - total_part)
    best_ref[0] = jnp.broadcast_to(jnp.max(best, axis=1, keepdims=True), best_ref.shape[1:])

def hist_and_best(bins, stats, spread):
    nodes, feats, slots = bins.shape
    st = stats.shape[1]
    chunks = slots // CH
    filled = jnp.any(bins[:, 0].reshape(nodes, chunks, CH) < B, axis=2)
    flags = filled.astype(jnp.int32).reshape(nodes * chunks)
    hist, best = pl.pallas_call(
        histogram_kernel,
        grid_spec=pltpu.PrefetchScalarGridSpec(
            num_scalar_prefetch=1,
            grid=(nodes,),
            in_specs=[pl.BlockSpec((1, feats, slots), lambda n, fl: (n, 0, 0)),
                      pl.BlockSpec((1, st, slots), lambda n, fl: (n, 0, 0))],
            out_specs=[pl.BlockSpec((1, feats, st, B), lambda n, fl: (n, 0, 0, 0)),
                       pl.BlockSpec((1, spread, 128), lambda n, fl: (n, 0, 0))]),
        out_shape=[jax.ShapeDtypeStruct((nodes, feats, st, B), jnp.float32),
                   jax.ShapeDtypeStruct((nodes, spread, 128), jnp.float32)])(flags, bins, stats)
    return hist, best


def running_rank(owned):
    rows, nodes = owned.shape
    blocks = rows // BLOCK
    ob = owned.reshape(blocks, BLOCK, nodes).astype(jnp.bfloat16)
    i = lax.broadcasted_iota(jnp.int32, (BLOCK, BLOCK), 0)
    j = lax.broadcasted_iota(jnp.int32, (BLOCK, BLOCK), 1)
    lower = (i >= j).astype(jnp.bfloat16)
    within = jnp.einsum("ij,bjn->bin", lower, ob, preferred_element_type=jnp.float32)
    totals = within[:, -1, :]
    a = lax.broadcasted_iota(jnp.int32, (blocks, blocks), 0)
    c = lax.broadcasted_iota(jnp.int32, (blocks, blocks), 1)
    before = (a > c).astype(jnp.float32)
    prefix = jnp.einsum("ac,cn->an", before, totals, precision=lax.Precision.HIGHEST)
    counts = within + prefix[:, None, :]
    mine = jnp.sum(counts * ob.astype(jnp.float32), axis=2).reshape(rows)
    return mine.astype(jnp.int32) - 1


def on_device(covariates, pseudo, honest, destination, node_slot):
    feat_count, row_count = covariates.shape
    node_devices = lax.axis_size("node")
    feat_devices = lax.axis_size("feat")
    node_total = node_slot.shape[0]
    node_local = node_total // node_devices
    capacity = 2 * row_count // node_total
    kept = honest == 0
    columns = lax.broadcasted_iota(jnp.int32, (1, node_total), 1)
    named = (destination == columns).astype(jnp.int32)
    target = jnp.sum(named * node_slot[None, :], axis=1)
    owned = ((target[:, None] == columns) & kept[:, None]).astype(jnp.int32)
    rank = running_rank(owned)
    slots = node_total * capacity
    position = jnp.where(kept, target * capacity + rank, slots)
    payload = jnp.concatenate([jnp.floor(covariates * B), pseudo], axis=0)
    payload_width = payload.shape[0]
    empty = jnp.concatenate(
        [jnp.full((feat_count, slots), B, jnp.bfloat16), jnp.zeros((payload_width - feat_count, slots), jnp.bfloat16)]
    )
    outgoing = empty.T.at[position].set(payload.T, mode="drop")
    outgoing = outgoing.reshape(node_devices, node_local * capacity, payload_width)
    arrived = lax.all_to_all(outgoing, "node", split_axis=0, concat_axis=0, tiled=True)
    arrived = arrived.reshape(node_devices, node_local, capacity, payload_width)
    arrived = jnp.transpose(arrived, (3, 1, 2, 0)).reshape(payload_width, node_local, capacity * node_devices)
    bin_table = arrived[:feat_count]
    bin_table = jnp.transpose(bin_table, (1, 0, 2))
    ones = jnp.ones((node_local, 1, arrived.shape[2]), jnp.bfloat16)
    statistics = jnp.concatenate([ones, jnp.transpose(arrived[feat_count:], (1, 0, 2))], axis=1)
    histogram, best_spread = hist_and_best(bin_table, statistics, feat_devices)
    gathered = lax.all_to_all(best_spread, "feat", split_axis=1, concat_axis=1, tiled=True)
    best_gain = jnp.max(gathered[:, :, 0], axis=1)
    return (histogram, best_gain)


def solution(mesh):
    placed = (P("feat", "node"), P(None, "node"), P("node"), P("node", None), P())
    return jax.shard_map(
        on_device,
        mesh=mesh,
        in_specs=placed,
        out_specs=(P("node", "feat", None, None), P("node")),
        check_vma=False,
    )
```

```python
import jax
import jax.numpy as jnp
from jax import lax
from jax.experimental import pallas as pl
from jax.experimental.pallas import tpu as pltpu
from jax.sharding import PartitionSpec as P

B = 256
BLOCK = 256
CH = 256


def histogram_kernel(flags_ref, bins_ref, stats_ref, hist_ref, best_ref):
    feats = bins_ref.shape[1]
    slots = bins_ref.shape[2]
    stat_count = stats_ref.shape[1]
    chunks = slots // CH
    node = pl.program_id(0)
    levels = lax.broadcasted_iota(jnp.int32, (B, CH), 0).astype(jnp.float32)
    best = jnp.full((1, B), -jnp.inf, jnp.float32)
    hist_ref[...] = jnp.zeros(hist_ref.shape, hist_ref.dtype)
    for k in range(chunks):

        @pl.when(flags_ref[node * chunks + k] > 0)
        def _():
            for f in range(feats):
                row = bins_ref[0, f:f + 1, k * CH:(k + 1) * CH].astype(jnp.float32)
                indicator = (levels == row).astype(jnp.bfloat16)
                hist_ref[0, f] += lax.dot_general(
                    stats_ref[0, :, k * CH:(k + 1) * CH], indicator, (((1,), (1,)), ((), ())),
                    preferred_element_type=jnp.float32)

    lane = lax.broadcasted_iota(jnp.int32, (stat_count, B), 1)
    for f in range(feats):
        left = hist_ref[0, f]
        shift = 1
        while shift < B:
            moved = pltpu.roll(left, shift, 1)
            left = left + jnp.where(lane >= shift, moved, 0.0)
            shift *= 2
        total = left[:, B - 1:B]
        right = total - left
        left_part = jnp.sum(left[1:] * left[1:], axis=0, keepdims=True) / (left[0:1] + 1.0)
        right_part = jnp.sum(right[1:] * right[1:], axis=0, keepdims=True) / (right[0:1] + 1.0)
        total_part = jnp.sum(total[1:] * total[1:], axis=0, keepdims=True) / (total[0:1] + 1.0)
        best = jnp.maximum(best, left_part + right_part - total_part)
    best_ref[...] = jnp.broadcast_to(jnp.max(best, axis=1, keepdims=True), best_ref.shape)

def hist_and_best(bins, stats, spread):
    nodes, feats, slots = bins.shape
    st = stats.shape[1]
    chunks = slots // CH
    filled = jnp.any(bins[:, 0].reshape(nodes, chunks, CH) < B, axis=2)
    flags = filled.astype(jnp.int32).reshape(nodes * chunks)
    hist, best = pl.pallas_call(
        histogram_kernel,
        grid_spec=pltpu.PrefetchScalarGridSpec(
            num_scalar_prefetch=1,
            grid=(nodes,),
            in_specs=[pl.BlockSpec((1, feats, slots), lambda n, fl: (n, 0, 0)),
                      pl.BlockSpec((1, st, slots), lambda n, fl: (n, 0, 0))],
            out_specs=[pl.BlockSpec((1, feats, st, B), lambda n, fl: (n, 0, 0, 0)),
                       pl.BlockSpec((spread, 1, 128), lambda n, fl: (0, 0, n))]),
        out_shape=[jax.ShapeDtypeStruct((nodes, feats, st, B), jnp.float32),
                   jax.ShapeDtypeStruct((spread, 1, nodes * 128), jnp.float32)])(flags, bins, stats)
    return hist, best


def running_rank(owned):
    rows, nodes = owned.shape
    blocks = rows // BLOCK
    ob = owned.reshape(blocks, BLOCK, nodes).astype(jnp.bfloat16)
    i = lax.broadcasted_iota(jnp.int32, (BLOCK, BLOCK), 0)
    j = lax.broadcasted_iota(jnp.int32, (BLOCK, BLOCK), 1)
    lower = (i >= j).astype(jnp.bfloat16)
    within = jnp.einsum("ij,bjn->bin", lower, ob, preferred_element_type=jnp.float32)
    totals = within[:, -1, :]
    a = lax.broadcasted_iota(jnp.int32, (blocks, blocks), 0)
    c = lax.broadcasted_iota(jnp.int32, (blocks, blocks), 1)
    before = (a > c).astype(jnp.float32)
    prefix = jnp.einsum("ac,cn->an", before, totals, precision=lax.Precision.HIGHEST)
    counts = within + prefix[:, None, :]
    mine = jnp.sum(counts * ob.astype(jnp.float32), axis=2).reshape(rows)
    return mine.astype(jnp.int32) - 1


def on_device(covariates, pseudo, honest, destination, node_slot):
    feat_count, row_count = covariates.shape
    node_devices = lax.axis_size("node")
    feat_devices = lax.axis_size("feat")
    node_total = node_slot.shape[0]
    node_local = node_total // node_devices
    capacity = 2 * row_count // node_total
    kept = honest == 0
    columns = lax.broadcasted_iota(jnp.int32, (1, node_total), 1)
    named = (destination == columns).astype(jnp.int32)
    target = jnp.sum(named * node_slot[None, :], axis=1)
    owned = ((target[:, None] == columns) & kept[:, None]).astype(jnp.int32)
    rank = running_rank(owned)
    slots = node_total * capacity
    position = jnp.where(kept, target * capacity + rank, slots)
    payload = jnp.concatenate([covariates, pseudo], axis=0)
    payload_width = payload.shape[0]
    empty = jnp.concatenate(
        [jnp.ones((feat_count, slots), jnp.bfloat16), jnp.zeros((payload_width - feat_count, slots), jnp.bfloat16)]
    )
    outgoing = empty.T.at[position].set(payload.T, mode="drop")
    outgoing = outgoing.reshape(node_devices, node_local * capacity, payload_width)
    arrived = lax.all_to_all(outgoing, "node", split_axis=0, concat_axis=0, tiled=True)
    arrived = arrived.reshape(node_devices, node_local, capacity, payload_width)
    arrived = jnp.transpose(arrived, (3, 1, 2, 0)).reshape(payload_width, node_local, capacity * node_devices)
    bin_table = jnp.floor(arrived[:feat_count] * B)
    bin_table = jnp.transpose(bin_table, (1, 0, 2))
    ones = jnp.ones((node_local, 1, arrived.shape[2]), jnp.bfloat16)
    statistics = jnp.concatenate([ones, jnp.transpose(arrived[feat_count:], (1, 0, 2))], axis=1)
    histogram, best_spread = hist_and_best(bin_table, statistics, feat_devices)
    gathered = lax.all_to_all(best_spread, "feat", split_axis=0, concat_axis=0, tiled=True)
    best_gain = jnp.max(gathered.reshape(feat_devices, node_local, 128)[:, :, 0], axis=0)
    return (histogram, best_gain)


def solution(mesh):
    placed = (P("feat", "node"), P(None, "node"), P("node"), P("node", None), P())
    return jax.shard_map(
        on_device,
        mesh=mesh,
        in_specs=placed,
        out_specs=(P("node", "feat", None, None), P("node")),
        check_vma=False,
    )
```

```python
import jax
import jax.numpy as jnp
from jax import lax
from jax.experimental import pallas as pl
from jax.experimental.pallas import tpu as pltpu
from jax.sharding import PartitionSpec as P

B = 256
BLOCK = 256
CH = 256


def histogram_kernel(flags_ref, bins_ref, stats_ref, hist_ref, best_ref):
    feats = bins_ref.shape[1]
    slots = bins_ref.shape[2]
    stat_count = stats_ref.shape[1]
    chunks = slots // CH
    node = pl.program_id(0)
    levels = lax.broadcasted_iota(jnp.int32, (B, CH), 0).astype(jnp.float32)
    best = jnp.full((1, B), -jnp.inf, jnp.float32)
    hist_ref[...] = jnp.zeros(hist_ref.shape, hist_ref.dtype)
    for k in range(chunks):

        @pl.when(flags_ref[node * chunks + k] > 0)
        def _():
            for f in range(feats):
                row = bins_ref[0, f:f + 1, k * CH:(k + 1) * CH].astype(jnp.float32)
                indicator = (levels == row).astype(jnp.bfloat16)
                hist_ref[0, f] += lax.dot_general(
                    stats_ref[0, :, k * CH:(k + 1) * CH], indicator, (((1,), (1,)), ((), ())),
                    preferred_element_type=jnp.float32)

    lane = lax.broadcasted_iota(jnp.int32, (stat_count, B), 1)
    for f in range(feats):
        left = hist_ref[0, f]
        shift = 1
        while shift < B:
            moved = pltpu.roll(left, shift, 1)
            left = left + jnp.where(lane >= shift, moved, 0.0)
            shift *= 2
        total = left[:, B - 1:B]
        right = total - left
        left_part = jnp.sum(left[1:] * left[1:], axis=0, keepdims=True) / (left[0:1] + 1.0)
        right_part = jnp.sum(right[1:] * right[1:], axis=0, keepdims=True) / (right[0:1] + 1.0)
        total_part = jnp.sum(total[1:] * total[1:], axis=0, keepdims=True) / (total[0:1] + 1.0)
        best = jnp.maximum(best, left_part + right_part - total_part)
    best_ref[...] = jnp.broadcast_to(jnp.max(best, axis=1, keepdims=True), best_ref.shape)

def hist_and_best(bins, stats, spread, flags):
    nodes, feats, slots = bins.shape
    st = stats.shape[1]
    chunks = slots // CH
    hist, best = pl.pallas_call(
        histogram_kernel,
        grid_spec=pltpu.PrefetchScalarGridSpec(
            num_scalar_prefetch=1,
            grid=(nodes,),
            in_specs=[pl.BlockSpec((1, feats, slots), lambda n, fl: (n, 0, 0)),
                      pl.BlockSpec((1, st, slots), lambda n, fl: (n, 0, 0))],
            out_specs=[pl.BlockSpec((1, feats, st, B), lambda n, fl: (n, 0, 0, 0)),
                       pl.BlockSpec((spread, 1, 128), lambda n, fl: (0, 0, n))]),
        out_shape=[jax.ShapeDtypeStruct((nodes, feats, st, B), jnp.float32),
                   jax.ShapeDtypeStruct((spread, 1, nodes * 128), jnp.float32)])(flags, bins, stats)
    return hist, best


def running_rank(owned):
    rows, nodes = owned.shape
    blocks = rows // BLOCK
    ob = owned.reshape(blocks, BLOCK, nodes).astype(jnp.bfloat16)
    i = lax.broadcasted_iota(jnp.int32, (BLOCK, BLOCK), 0)
    j = lax.broadcasted_iota(jnp.int32, (BLOCK, BLOCK), 1)
    lower = (i >= j).astype(jnp.bfloat16)
    within = jnp.einsum("ij,bjn->bin", lower, ob, preferred_element_type=jnp.float32)
    totals = within[:, -1, :]
    a = lax.broadcasted_iota(jnp.int32, (blocks, blocks), 0)
    c = lax.broadcasted_iota(jnp.int32, (blocks, blocks), 1)
    before = (a > c).astype(jnp.float32)
    prefix = jnp.einsum("ac,cn->an", before, totals, precision=lax.Precision.HIGHEST)
    counts = within + prefix[:, None, :]
    mine = jnp.sum(counts * ob.astype(jnp.float32), axis=2).reshape(rows)
    return mine.astype(jnp.int32) - 1


def on_device(covariates, pseudo, honest, destination, node_slot):
    feat_count, row_count = covariates.shape
    node_devices = lax.axis_size("node")
    feat_devices = lax.axis_size("feat")
    node_total = node_slot.shape[0]
    node_local = node_total // node_devices
    capacity = 2 * row_count // node_total
    kept = honest == 0
    columns = lax.broadcasted_iota(jnp.int32, (1, node_total), 1)
    named = (destination == columns).astype(jnp.int32)
    target = jnp.sum(named * node_slot[None, :], axis=1)
    owned = ((target[:, None] == columns) & kept[:, None]).astype(jnp.int32)
    rank = running_rank(owned)
    slots = node_total * capacity
    position = jnp.where(kept, target * capacity + rank, slots)
    payload = jnp.concatenate([covariates, pseudo], axis=0)
    payload_width = payload.shape[0]
    empty = jnp.concatenate(
        [jnp.ones((feat_count, slots), jnp.bfloat16), jnp.zeros((payload_width - feat_count, slots), jnp.bfloat16)]
    )
    outgoing = empty.T.at[position].set(payload.T, mode="drop")
    outgoing = outgoing.reshape(node_devices, node_local * capacity, payload_width)
    arrived = lax.all_to_all(outgoing, "node", split_axis=0, concat_axis=0, tiled=True)
    arrived = arrived.reshape(node_devices, node_local, capacity, payload_width)
    firsts = arrived[:, :, :, 0].reshape(node_devices, node_local * capacity * node_devices // CH, CH // node_devices)
    flags = jnp.any(firsts < B, axis=(0, 2)).astype(jnp.int32)
    arrived = jnp.transpose(arrived, (3, 1, 2, 0)).reshape(payload_width, node_local, capacity * node_devices)
    bin_table = jnp.floor(arrived[:feat_count] * B)
    bin_table = jnp.transpose(bin_table, (1, 0, 2))
    ones = jnp.ones((node_local, 1, arrived.shape[2]), jnp.bfloat16)
    statistics = jnp.concatenate([ones, jnp.transpose(arrived[feat_count:], (1, 0, 2))], axis=1)
    histogram, best_spread = hist_and_best(bin_table, statistics, feat_devices, flags)
    gathered = lax.all_to_all(best_spread, "feat", split_axis=0, concat_axis=0, tiled=True)
    best_gain = jnp.max(gathered.reshape(feat_devices, node_local, 128)[:, :, 0], axis=0)
    return (histogram, best_gain)


def solution(mesh):
    placed = (P("feat", "node"), P(None, "node"), P("node"), P("node", None), P())
    return jax.shard_map(
        on_device,
        mesh=mesh,
        in_specs=placed,
        out_specs=(P("node", "feat", None, None), P("node")),
        check_vma=False,
    )
```

```python
import jax
import jax.numpy as jnp
from jax import lax
from jax.experimental import pallas as pl
from jax.experimental.pallas import tpu as pltpu
from jax.sharding import PartitionSpec as P

B = 256
BLOCK = 256
CH = 256


def histogram_kernel(flags_ref, bins_ref, stats_ref, hist_ref, best_ref):
    feats = bins_ref.shape[1]
    slots = bins_ref.shape[2]
    stat_count = stats_ref.shape[1]
    chunks = slots // CH
    node = pl.program_id(0)
    levels = lax.broadcasted_iota(jnp.int32, (B, CH), 0).astype(jnp.float32)
    best = jnp.full((1, B), -jnp.inf, jnp.float32)
    hist_ref[...] = jnp.zeros(hist_ref.shape, hist_ref.dtype)
    for k in range(chunks):

        @pl.when(flags_ref[node * chunks + k] > 0)
        def _():
            for f in range(feats):
                row = bins_ref[0, f:f + 1, k * CH:(k + 1) * CH].astype(jnp.float32)
                indicator = (levels == row).astype(jnp.bfloat16)
                hist_ref[0, f] += lax.dot_general(
                    stats_ref[0, :, k * CH:(k + 1) * CH], indicator, (((1,), (1,)), ((), ())),
                    preferred_element_type=jnp.float32)

    lane = lax.broadcasted_iota(jnp.int32, (stat_count, B), 1)
    for f in range(feats):
        left = hist_ref[0, f]
        shift = 1
        while shift < B:
            moved = pltpu.roll(left, shift, 1)
            left = left + jnp.where(lane >= shift, moved, 0.0)
            shift *= 2
        total = left[:, B - 1:B]
        right = total - left
        left_part = jnp.sum(left[1:] * left[1:], axis=0, keepdims=True) / (left[0:1] + 1.0)
        right_part = jnp.sum(right[1:] * right[1:], axis=0, keepdims=True) / (right[0:1] + 1.0)
        total_part = jnp.sum(total[1:] * total[1:], axis=0, keepdims=True) / (total[0:1] + 1.0)
        best = jnp.maximum(best, left_part + right_part - total_part)
    best_ref[...] = jnp.broadcast_to(jnp.max(best, axis=1, keepdims=True), best_ref.shape)

def hist_and_best(bins, stats, spread):
    nodes, feats, slots = bins.shape
    st = stats.shape[1]
    chunks = slots // CH
    filled = jnp.any(bins[:, 0].reshape(nodes, chunks, CH) < B, axis=2)
    flags = filled.astype(jnp.int32).reshape(nodes * chunks)
    hist, best = pl.pallas_call(
        histogram_kernel,
        grid_spec=pltpu.PrefetchScalarGridSpec(
            num_scalar_prefetch=1,
            grid=(nodes,),
            in_specs=[pl.BlockSpec((1, feats, slots), lambda n, fl: (n, 0, 0)),
                      pl.BlockSpec((1, st, slots), lambda n, fl: (n, 0, 0))],
            out_specs=[pl.BlockSpec((1, feats, st, B), lambda n, fl: (n, 0, 0, 0)),
                       pl.BlockSpec((spread, 1, 128), lambda n, fl: (0, 0, n))]),
        out_shape=[jax.ShapeDtypeStruct((nodes, feats, st, B), jnp.float32),
                   jax.ShapeDtypeStruct((spread, 1, nodes * 128), jnp.float32)])(flags, bins, stats)
    return hist, best


def running_rank(owned):
    rows, nodes = owned.shape
    blocks = rows // BLOCK
    ob = owned.reshape(blocks, BLOCK, nodes).astype(jnp.bfloat16)
    i = lax.broadcasted_iota(jnp.int32, (BLOCK, BLOCK), 0)
    j = lax.broadcasted_iota(jnp.int32, (BLOCK, BLOCK), 1)
    lower = (i >= j).astype(jnp.bfloat16)
    within = jnp.einsum("ij,bjn->bin", lower, ob, preferred_element_type=jnp.float32)
    totals = within[:, -1, :]
    a = lax.broadcasted_iota(jnp.int32, (blocks, blocks), 0)
    c = lax.broadcasted_iota(jnp.int32, (blocks, blocks), 1)
    before = (a > c).astype(jnp.float32)
    prefix = jnp.einsum("ac,cn->an", before, totals, precision=lax.Precision.HIGHEST)
    counts = within + prefix[:, None, :]
    mine = jnp.sum(counts * ob.astype(jnp.float32), axis=2).reshape(rows)
    return mine.astype(jnp.int32) - 1


def on_device(covariates, pseudo, honest, destination, node_slot):
    feat_count, row_count = covariates.shape
    node_devices = lax.axis_size("node")
    feat_devices = lax.axis_size("feat")
    node_total = node_slot.shape[0]
    node_local = node_total // node_devices
    capacity = 2 * row_count // node_total
    kept = honest == 0
    columns = lax.broadcasted_iota(jnp.int32, (1, node_total), 1)
    named = (destination == columns).astype(jnp.int32)
    target = jnp.sum(named * node_slot[None, :], axis=1)
    owned = ((target[:, None] == columns) & kept[:, None]).astype(jnp.int32)
    rank = running_rank(owned)
    slots = node_total * capacity
    position = jnp.where(kept, target * capacity + rank, slots)
    weight_row = jnp.ones((1, row_count), jnp.bfloat16)
    payload = jnp.concatenate([covariates, weight_row, pseudo], axis=0)
    payload_width = payload.shape[0]
    empty = jnp.concatenate(
        [jnp.ones((feat_count, slots), jnp.bfloat16), jnp.zeros((payload_width - feat_count, slots), jnp.bfloat16)]
    )
    outgoing = empty.T.at[position].set(payload.T, mode="drop")
    outgoing = outgoing.reshape(node_devices, node_local * capacity, payload_width)
    arrived = lax.all_to_all(outgoing, "node", split_axis=0, concat_axis=0, tiled=True)
    arrived = arrived.reshape(node_devices, node_local, capacity, payload_width)
    arrived = jnp.transpose(arrived, (3, 1, 2, 0)).reshape(payload_width, node_local, capacity * node_devices)
    bin_table = jnp.floor(arrived[:feat_count] * B)
    bin_table = jnp.transpose(bin_table, (1, 0, 2))
    statistics = jnp.transpose(arrived[feat_count:], (1, 0, 2))
    histogram, best_spread = hist_and_best(bin_table, statistics, feat_devices)
    gathered = lax.all_to_all(best_spread, "feat", split_axis=0, concat_axis=0, tiled=True)
    best_gain = jnp.max(gathered.reshape(feat_devices, node_local, 128)[:, :, 0], axis=0)
    return (histogram, best_gain)


def solution(mesh):
    placed = (P("feat", "node"), P(None, "node"), P("node"), P("node", None), P())
    return jax.shard_map(
        on_device,
        mesh=mesh,
        in_specs=placed,
        out_specs=(P("node", "feat", None, None), P("node")),
        check_vma=False,
    )
```

```python
import jax
import jax.numpy as jnp
from jax import lax
from jax.experimental import pallas as pl
from jax.experimental.pallas import tpu as pltpu
from jax.sharding import PartitionSpec as P

B = 256
BLOCK = 256
CH = 256


def histogram_kernel(flags_ref, bins_ref, stats_ref, hist_ref, best_ref):
    feats = bins_ref.shape[1]
    slots = bins_ref.shape[2]
    stat_count = stats_ref.shape[1]
    chunks = slots // CH
    node = pl.program_id(0)
    levels = lax.broadcasted_iota(jnp.int32, (B, CH), 0).astype(jnp.float32)
    best = jnp.full((1, B), -jnp.inf, jnp.float32)
    hist_ref[...] = jnp.zeros(hist_ref.shape, hist_ref.dtype)
    for k in range(chunks):

        @pl.when(flags_ref[node * chunks + k] > 0)
        def _():
            for f in range(feats):
                row = bins_ref[0, f:f + 1, k * CH:(k + 1) * CH].astype(jnp.float32)
                indicator = (levels == row).astype(jnp.bfloat16)
                hist_ref[0, f] += lax.dot_general(
                    stats_ref[0, :, k * CH:(k + 1) * CH], indicator, (((1,), (1,)), ((), ())),
                    preferred_element_type=jnp.float32)

    lane = lax.broadcasted_iota(jnp.int32, (stat_count, B), 1)
    for f in range(feats):
        left = hist_ref[0, f]
        shift = 1
        while shift < B:
            moved = pltpu.roll(left, shift, 1)
            left = left + jnp.where(lane >= shift, moved, 0.0)
            shift *= 2
        total = left[:, B - 1:B]
        right = total - left
        left_part = jnp.sum(left[1:] * left[1:], axis=0, keepdims=True) / (left[0:1] + 1.0)
        right_part = jnp.sum(right[1:] * right[1:], axis=0, keepdims=True) / (right[0:1] + 1.0)
        total_part = jnp.sum(total[1:] * total[1:], axis=0, keepdims=True) / (total[0:1] + 1.0)
        best = jnp.maximum(best, left_part + right_part - total_part)
    best_ref[...] = jnp.broadcast_to(jnp.max(best, axis=1, keepdims=True), best_ref.shape)

def hist_and_best(bins, stats, spread):
    nodes, feats, slots = bins.shape
    st = stats.shape[1]
    chunks = slots // CH
    filled = jnp.any(bins[:, 0].reshape(nodes, chunks, CH) < B, axis=2)
    flags = filled.astype(jnp.int32).reshape(nodes * chunks)
    hist, best = pl.pallas_call(
        histogram_kernel,
        grid_spec=pltpu.PrefetchScalarGridSpec(
            num_scalar_prefetch=1,
            grid=(nodes,),
            in_specs=[pl.BlockSpec((1, feats, slots), lambda n, fl: (n, 0, 0)),
                      pl.BlockSpec((1, st, slots), lambda n, fl: (n, 0, 0))],
            out_specs=[pl.BlockSpec((1, feats, st, B), lambda n, fl: (n, 0, 0, 0)),
                       pl.BlockSpec((spread, 1, 128), lambda n, fl: (0, 0, n))]),
        out_shape=[jax.ShapeDtypeStruct((nodes, feats, st, B), jnp.float32),
                   jax.ShapeDtypeStruct((spread, 1, nodes * 128), jnp.float32)])(flags, bins, stats)
    return hist, best


def running_rank(owned):
    rows, nodes = owned.shape
    blocks = rows // BLOCK
    ob = owned.reshape(blocks, BLOCK, nodes).astype(jnp.bfloat16)
    i = lax.broadcasted_iota(jnp.int32, (BLOCK, BLOCK), 0)
    j = lax.broadcasted_iota(jnp.int32, (BLOCK, BLOCK), 1)
    lower = (i >= j).astype(jnp.bfloat16)
    within = jnp.einsum("ij,bjn->bin", lower, ob, preferred_element_type=jnp.float32)
    totals = within[:, -1, :]
    a = lax.broadcasted_iota(jnp.int32, (blocks, blocks), 0)
    c = lax.broadcasted_iota(jnp.int32, (blocks, blocks), 1)
    before = (a > c).astype(jnp.float32)
    prefix = jnp.einsum("ac,cn->an", before, totals, precision=lax.Precision.HIGHEST)
    counts = within + prefix[:, None, :]
    mine = jnp.sum(counts * ob.astype(jnp.float32), axis=2).reshape(rows)
    return mine.astype(jnp.int32) - 1


def on_device(covariates, pseudo, honest, destination, node_slot):
    feat_count, row_count = covariates.shape
    node_devices = lax.axis_size("node")
    feat_devices = lax.axis_size("feat")
    node_total = node_slot.shape[0]
    node_local = node_total // node_devices
    capacity = 2 * row_count // node_total
    kept = honest == 0
    columns = lax.broadcasted_iota(jnp.int32, (1, node_total), 1)
    named = (destination == columns).astype(jnp.int32)
    target = jnp.sum(named * node_slot[None, :], axis=1)
    owned = ((target[:, None] == columns) & kept[:, None]).astype(jnp.int32)
    rank = running_rank(owned)
    slots = node_total * capacity
    position = jnp.where(kept, target * capacity + rank, slots)
    payload = jnp.concatenate([jnp.floor(covariates * B), pseudo], axis=0)
    payload_width = payload.shape[0]
    empty = jnp.concatenate(
        [jnp.full((feat_count, slots), B, jnp.bfloat16), jnp.zeros((payload_width - feat_count, slots), jnp.bfloat16)]
    )
    outgoing = empty.T.at[position].set(payload.T, mode="drop")
    outgoing = outgoing.reshape(node_devices, node_local * capacity, payload_width)
    arrived = lax.all_to_all(outgoing, "node", split_axis=0, concat_axis=0, tiled=True)
    arrived = arrived.reshape(node_devices, node_local, capacity, payload_width)
    arrived = jnp.transpose(arrived, (3, 1, 2, 0)).reshape(payload_width, node_local, capacity * node_devices)
    bin_table = arrived[:feat_count]
    bin_table = jnp.transpose(bin_table, (1, 0, 2))
    ones = jnp.ones((node_local, 1, arrived.shape[2]), jnp.bfloat16)
    statistics = jnp.concatenate([ones, jnp.transpose(arrived[feat_count:], (1, 0, 2))], axis=1)
    histogram, best_spread = hist_and_best(bin_table, statistics, feat_devices)
    gathered = lax.all_to_all(best_spread, "feat", split_axis=0, concat_axis=0, tiled=True)
    best_gain = jnp.max(gathered.reshape(feat_devices, node_local, 128)[:, :, 0], axis=0)
    return (histogram, best_gain)


def solution(mesh):
    placed = (P("feat", "node"), P(None, "node"), P("node"), P("node", None), P())
    return jax.shard_map(
        on_device,
        mesh=mesh,
        in_specs=placed,
        out_specs=(P("node", "feat", None, None), P("node")),
        check_vma=False,
    )
```
